256 devices in a mesh: dp: 64 (over y, z_lo, x), tensor: 4 (over z_hi, core).
Axes of the slice: x: 4, y: 4, z: 8 (z_hi: 2, z_lo: 4; z = z_hi * 4 + z_lo), core: 2. Of those that a mesh axis runs over, the one named last changes fastest.
Arguments:
- tokens: bfloat16 [16384, 8192], P('dp', 'tensor'), may hold values from -160 to 160
- weights: bfloat16 [3, 512, 32, 256], P(None, None, 'tensor'), may hold values from -0.25 to 0.25
- cotangent: bfloat16 [16384, 8192], P('dp', 'tensor'), may hold values from -6 to 6
Outputs:
- mixed: bfloat16 [16384, 8192], P('dp', 'tensor')
- token_grads: bfloat16 [16384, 8192], P('dp', 'tensor')
- weight_grads: float32 [3, 512, 32, 256], P(None, 'dp', 'tensor')
The draws below stay inside these ranges and needn't reach their ends.
All inputs are finite; a program needn't handle non-finite values.
Results may differ from the reference program's by a relative error of at most 0.0014.
The reference program's roundings to bfloat16 on the way count: a program that leaves them out, or rounds other values in their place, can miss the bound.
Values may be sent and summed in bfloat16 or wider, within the bound.
No kernel may reach another device: no remote copies, remote signals or barrier semaphores. Data moves between devices by JAX's collectives and lax.ppermute only.
A program may use at most 128 MiB of HBM per device.

```python
import math
import jax
import jax.numpy as jnp
from jax import lax

D = 8192
BLK = 256
FACTORS = 3
TOK_DEV = 256
NBLK = 32
TOKENS = 16384
N_DP = 64


def draw_tokens(key, part):
    key_base, key_rows, key_cols = jax.random.split(key, 3)
    cols = jnp.exp(jax.random.uniform(key_cols, (1, D), jnp.float32, 0.0, math.log(10.0)))
    trend = jnp.exp(math.log(3.0) * jnp.arange(D, dtype=jnp.float32) / D)[None, :]
    rows = jnp.exp(jax.random.uniform(key_rows, (TOKENS, 1), jnp.float32, 0.0, math.log(10.0)))
    base = jnp.clip(jax.random.normal(key_base, (TOKENS, D), jnp.float32), -4.0, 4.0)
    return (base * rows * cols * trend * 0.1).astype(jnp.bfloat16)


def shard_levels(rng, dims, shards, smallest, top_value):
    def one(axis_at, parts):
        draws = jax.random.uniform(jax.random.fold_in(jax.random.fold_in(rng, 6), axis_at), (parts,), jnp.float32, smallest / len(shards), top_value / len(shards))
        return jnp.repeat(jnp.exp(draws), dims[axis_at] // parts).reshape((-1,) + (1,) * (len(dims) - axis_at - 1))

    gain = one(*shards[0])
    for cut in shards[1:]:
        gain = gain * one(*cut)
    return gain


def bell_draw(rng, dims, spread, most, cuts=(), kind=jnp.bfloat16):
    drawn = spread * jax.random.normal(rng, dims, jnp.float32)
    if cuts:
        drawn = drawn * shard_levels(rng, dims, cuts, -0.22, 0.18)
    return jnp.clip(drawn, -most, most).astype(kind)


def setup_inputs(seed: int = 0) -> dict:
    keys = jax.random.split(jax.random.key(seed), 4)
    tokens = draw_tokens(jax.random.fold_in(keys[3], 71), 0)
    weights = bell_draw(keys[1], (FACTORS, 2 * BLK, NBLK, BLK), (2 * BLK) ** -0.5, 0.25, ((2, 4),))
    cotangent = bell_draw(keys[2], (TOKENS, D), 1.0, 6.0, ((0, 64), (1, 4)))
    return {"tokens": tokens, "weights": weights, "cotangent": cotangent}


root_half = 0.7071067811865476
pdf_scale = 0.3989422804014327
epsilon = 1e-06

def gelu_value(value):
    return value * (0.5 * (1.0 + lax.erf(value * root_half)))

def gelu_slope(value):
    return 0.5 * (1.0 + lax.erf(value * root_half)) + value * jnp.exp(-0.5 * value * value) * pdf_scale

def local_partner(blocks, stride):
    tok_rows, block_count, width = blocks.shape
    folded = blocks.reshape(tok_rows, block_count // (2 * stride), 2, stride, width)
    return jnp.flip(folded, axis=2).reshape(tok_rows, block_count, width)

def layer_pass(tok_block, cot_block, weights_f32, block_bits):
    tok_rows = tok_block.shape[0]
    tokens_f32 = tok_block.astype(jnp.float32)
    square_sum = lax.optimization_barrier(jnp.sum(tokens_f32 * tokens_f32, axis=1))
    inv_rms = lax.rsqrt(square_sum / D + epsilon)[:, None]
    normed = tokens_f32 * inv_rms
    hidden = normed.astype(jnp.bfloat16).reshape(tok_rows, NBLK, BLK)
    stored_inputs = []
    stored_preact = []
    preact = None
    for factor in range(FACTORS):
        stride = 1 << block_bits - FACTORS + factor
        partner = local_partner(hidden, stride)
        layer_weights = weights_f32[factor]
        preact = jnp.einsum('tbc,cbd->tbd', hidden.astype(jnp.float32), layer_weights[:BLK])
        preact = preact + jnp.einsum('tbc,cbd->tbd', partner.astype(jnp.float32), layer_weights[BLK:])
        stored_inputs.append((hidden, partner))
        stored_preact.append(preact)
        if factor < FACTORS - 1:
            hidden = gelu_value(preact).astype(jnp.bfloat16)
    mixed = (tokens_f32 + preact.reshape(tok_rows, D)).astype(jnp.bfloat16)
    grad_pre = cot_block.reshape(tok_rows, NBLK, BLK)
    grad_terms = []
    grad_hidden = None
    for factor in reversed(range(FACTORS)):
        stride = 1 << block_bits - FACTORS + factor
        hidden, partner = stored_inputs[factor]
        joined = jnp.concatenate([hidden, partner], axis=2).astype(jnp.float32)
        grad_f32 = grad_pre.astype(jnp.float32)
        grad_terms.append(jnp.einsum('tbc,tbd->cbd', joined, grad_f32))
        layer_weights = weights_f32[factor]
        near_term = jnp.einsum('tbd,cbd->tbc', grad_f32, layer_weights[:BLK])
        far_term = jnp.einsum('tbd,cbd->tbc', grad_f32, layer_weights[BLK:])
        grad_hidden = near_term + local_partner(far_term, stride)
        if factor > 0:
            grad_pre = (grad_hidden * gelu_slope(stored_preact[factor - 1])).astype(jnp.bfloat16)
    flat = grad_hidden.reshape(tok_rows, D)
    inner_sum = lax.optimization_barrier(jnp.sum(flat * normed, axis=1))
    token_grads = (cot_block.astype(jnp.float32) + inv_rms * (flat - normed * (inner_sum / D)[:, None])).astype(jnp.bfloat16)
    return (mixed, token_grads, jnp.stack(grad_terms[::-1]))

def reference(tokens, weights, cotangent):
    block_bits = NBLK.bit_length() - 1
    weights_f32 = weights.astype(jnp.float32)
    tok_groups = tokens.reshape(N_DP, TOK_DEV, D)
    cot_groups = cotangent.reshape(N_DP, TOK_DEV, D)

    def one_group(totals, pair):
        tok_block, cot_block = pair
        mixed, token_grads, grad_terms = layer_pass(tok_block, cot_block, weights_f32, block_bits)
        return (totals + grad_terms, (mixed, token_grads))
    initial = jnp.zeros((FACTORS, 2 * BLK, NBLK, BLK), jnp.float32)
    totals, outputs = lax.scan(one_group, initial, (tok_groups, cot_groups))
    mixed, token_grads = outputs
    weight_grads = totals * (1.0 / math.sqrt(TOKENS))
    return (mixed.reshape(TOKENS, D), token_grads.reshape(TOKENS, D), weight_grads)
```

```python
import math

import jax
import jax.numpy as jnp
from jax import lax
from jax.sharding import Mesh, PartitionSpec as P

D = 8192
BLK = 256
FACTORS = 3


root_half = 0.7071067811865476
pdf_scale = 0.3989422804014327
epsilon = 1e-06


def swapped(x, axis, stride):
    return lax.ppermute(x, axis, [(i, i ^ 1 << stride) for i in range(lax.axis_size(axis))])


def tensor_sum(x):
    for bit in range(lax.axis_size("tensor").bit_length() - 1):
        x = x + swapped(x, "tensor", bit)
    return x


def staged_scatter(grads):
    factors, rows = grads.shape[:2]
    ny, nz, nx = (lax.axis_size(a) for a in ("dy", "dz", "dx"))
    rest = grads.shape[2:]
    share = rows // (ny * nz * nx)
    g = grads.reshape((factors, ny, nz, nx, share) + rest)
    g = jnp.transpose(g, (3, 1, 2, 0) + tuple(range(4, g.ndim)))
    lanes = rest[-1]
    for axis, size in (("dx", nx), ("dy", ny), ("dz", nz)):
        g = g.reshape(size, -1, lanes)
        g = lax.psum_scatter(g, axis, scatter_dimension=0, tiled=True)
    return g.reshape((factors, share) + rest)


def gelu_value(value):
    return value * (0.5 * (1.0 + lax.erf(value * root_half)))


def gelu_slope(value):
    return (
        0.5 * (1.0 + lax.erf(value * root_half)) + value * jnp.exp(-0.5 * value * value) * pdf_scale
    )


def local_partner(blocks, stride):
    tok_rows, block_count, width = blocks.shape
    folded = blocks.reshape(tok_rows, block_count // (2 * stride), 2, stride, width)
    return jnp.flip(folded, axis=2).reshape(tok_rows, block_count, width)


def apply_factor(hidden, partner, layer_weights):
    preact = jnp.einsum(
        "tbc,cbd->tbd", hidden, layer_weights[:BLK], preferred_element_type=jnp.float32
    )
    return preact + jnp.einsum(
        "tbc,cbd->tbd", partner, layer_weights[BLK:], preferred_element_type=jnp.float32
    )


def shards(tokens, weights, cotangent):
    tok_rows, local_width = tokens.shape
    blocks_dev = local_width // BLK
    block_bits = (D // BLK).bit_length() - 1
    device_bits = blocks_dev.bit_length() - 1
    data_size = lax.axis_size(("dy", "dz", "dx"))
    grad_scale = 1.0 / math.sqrt(tok_rows * data_size)
    tokens_f32 = tokens.astype(jnp.float32)
    square_sum = tensor_sum(jnp.sum(tokens_f32 * tokens_f32, axis=1))
    inv_rms = lax.rsqrt(square_sum / D + epsilon)[:, None]
    normed = tokens_f32 * inv_rms
    hidden = normed.astype(jnp.bfloat16).reshape(tok_rows, blocks_dev, BLK)
    stored_inputs = []
    stored_preact = []
    preact = None
    for factor in range(FACTORS):
        bit_index = block_bits - FACTORS + factor
        stride = 1 << bit_index
        if stride < blocks_dev:
            partner = local_partner(hidden, stride)
        else:
            partner = swapped(hidden, "tensor", bit_index - device_bits)
        preact = apply_factor(hidden, partner, weights[factor])
        stored_inputs.append((hidden, partner))
        stored_preact.append(preact)
        if factor < FACTORS - 1:
            hidden = gelu_value(preact).astype(jnp.bfloat16)
    mixed = (tokens_f32 + preact.reshape(tok_rows, local_width)).astype(jnp.bfloat16)
    grad_pre = cotangent.reshape(tok_rows, blocks_dev, BLK)
    grad_terms = []
    grad_hidden = None
    for factor in reversed(range(FACTORS)):
        bit_index = block_bits - FACTORS + factor
        stride = 1 << bit_index
        kept_hidden, kept_partner = stored_inputs[factor]
        joined = jnp.concatenate([kept_hidden, kept_partner], axis=2)
        grad_terms.append(
            jnp.einsum("tbc,tbd->cbd", joined, grad_pre, preferred_element_type=jnp.float32)
            * grad_scale
        )
        layer_weights = weights[factor]
        near_term = jnp.einsum(
            "tbd,cbd->tbc", grad_pre, layer_weights[:BLK], preferred_element_type=jnp.float32
        )
        far_term = jnp.einsum(
            "tbd,cbd->tbc", grad_pre, layer_weights[BLK:], preferred_element_type=jnp.float32
        )
        if stride < blocks_dev:
            arrived = local_partner(far_term, stride)
        else:
            arrived = swapped(far_term, "tensor", bit_index - device_bits)
        grad_hidden = near_term + arrived
        if factor > 0:
            previous = stored_preact[factor - 1]
            grad_pre = (grad_hidden * gelu_slope(previous)).astype(jnp.bfloat16)
    flat = grad_hidden.reshape(tok_rows, local_width)
    inner_sum = tensor_sum(jnp.sum(flat * normed, axis=1))
    token_grads = (
        cotangent.astype(jnp.float32) + inv_rms * (flat - normed * (inner_sum / D)[:, None])
    ).astype(jnp.bfloat16)
    weight_grads = staged_scatter(jnp.stack(grad_terms[::-1]))
    return (mixed, token_grads, weight_grads)


def solution(mesh):
    ny, nz, nx = 4, 4, 4
    fine = Mesh(
        mesh.devices.reshape(ny, nz, nx, mesh.shape["tensor"]), ("dy", "dz", "dx", "tensor")
    )
    dp = ("dy", "dz", "dx")
    return jax.shard_map(
        shards,
        mesh=fine,
        in_specs=(P(dp, "tensor"), P(None, None, "tensor", None), P(dp, "tensor")),
        out_specs=(P(dp, "tensor"), P(dp, "tensor"), P(None, dp, "tensor", None)),
        check_vma=False,
    )
```

```python
import math

import jax
import jax.numpy as jnp
from jax import lax
from jax.sharding import Mesh, PartitionSpec as P

D = 8192
BLK = 256
FACTORS = 3


root_half = 0.7071067811865476
pdf_scale = 0.3989422804014327
epsilon = 1e-06


def swapped(x, axis, stride):
    return lax.ppermute(x, axis, [(i, i ^ 1 << stride) for i in range(lax.axis_size(axis))])


def tensor_sum(x):
    for bit in range(lax.axis_size("tensor").bit_length() - 1):
        x = x + swapped(x, "tensor", bit)
    return x


def scatter_first(grads):
    rows = grads.shape[0]
    ny, nz, nx = (lax.axis_size(a) for a in ("dy", "dz", "dx"))
    rest = grads.shape[1:]
    share = rows // (ny * nz * nx)
    g = grads.reshape((ny, nz, nx, share) + rest)
    g = jnp.moveaxis(g, 2, 0).reshape(nx, -1, rest[-1])
    g = lax.psum_scatter(g, "dx", scatter_dimension=0, tiled=True)
    return g.reshape((ny, nz, share) + rest)


def scatter_rest(parts):
    ny, nz, share = parts[0].shape[:3]
    rest = parts[0].shape[3:]
    g = jnp.stack(parts, axis=2)
    for axis, size in (("dy", ny), ("dz", nz)):
        g = g.reshape(size, -1, rest[-1])
        g = lax.psum_scatter(g, axis, scatter_dimension=0, tiled=True)
    return g.reshape((len(parts), share) + rest)


def partner_rows(rows):
    pieces = lax.axis_size(("dy", "dx"))
    piece = rows.shape[0] // pieces
    mine = lax.axis_index("dy") * lax.axis_size("dx") + lax.axis_index("dx")
    part = lax.dynamic_slice_in_dim(rows, mine * piece, piece, axis=0)
    part = swapped(part, "tensor", 1)
    return lax.all_gather(part, ("dy", "dx"), axis=0, tiled=True)


def gelu_value(value):
    return value * (0.5 * (1.0 + lax.erf(value * root_half)))


def gelu_slope(value):
    return (
        0.5 * (1.0 + lax.erf(value * root_half)) + value * jnp.exp(-0.5 * value * value) * pdf_scale
    )


def local_partner(blocks, stride):
    tok_rows, block_count, width = blocks.shape
    folded = blocks.reshape(tok_rows, block_count // (2 * stride), 2, stride, width)
    return jnp.flip(folded, axis=2).reshape(tok_rows, block_count, width)


def apply_factor(hidden, partner, layer_weights):
    preact = jnp.einsum(
        "tbc,cbd->tbd", hidden, layer_weights[:BLK], preferred_element_type=jnp.float32
    )
    return preact + jnp.einsum(
        "tbc,cbd->tbd", partner, layer_weights[BLK:], preferred_element_type=jnp.float32
    )


def shards(tokens, weights, cotangent):
    tok_rows, local_width = tokens.shape
    blocks_dev = local_width // BLK
    block_bits = (D // BLK).bit_length() - 1
    device_bits = blocks_dev.bit_length() - 1
    data_size = lax.axis_size(("dy", "dz", "dx"))
    grad_scale = 1.0 / math.sqrt(tok_rows * data_size)
    tokens_f32 = tokens.astype(jnp.float32)
    square_sum = tensor_sum(jnp.sum(tokens_f32 * tokens_f32, axis=1))
    inv_rms = lax.rsqrt(square_sum / D + epsilon)[:, None]
    normed = tokens_f32 * inv_rms
    hidden = normed.astype(jnp.bfloat16).reshape(tok_rows, blocks_dev, BLK)
    stored_inputs = []
    stored_preact = []
    preact = None
    for factor in range(FACTORS):
        bit_index = block_bits - FACTORS + factor
        stride = 1 << bit_index
        if stride < blocks_dev:
            partner = local_partner(hidden, stride)
        else:
            partner = swapped(hidden, "tensor", bit_index - device_bits)
        preact = apply_factor(hidden, partner, weights[factor])
        stored_inputs.append((hidden, partner))
        stored_preact.append(preact)
        if factor < FACTORS - 1:
            hidden = gelu_value(preact).astype(jnp.bfloat16)
    mixed = (tokens_f32 + preact.reshape(tok_rows, local_width)).astype(jnp.bfloat16)
    grad_pre = cotangent.reshape(tok_rows, blocks_dev, BLK)
    grad_terms = []
    grad_hidden = None
    for factor in reversed(range(FACTORS)):
        bit_index = block_bits - FACTORS + factor
        stride = 1 << bit_index
        kept_hidden, kept_partner = stored_inputs[factor]
        joined = jnp.concatenate([kept_hidden, kept_partner], axis=2)
        grad_terms.append(
            scatter_first(
                jnp.einsum("tbc,tbd->cbd", joined, grad_pre, preferred_element_type=jnp.float32)
                * grad_scale
            )
        )
        layer_weights = weights[factor]
        near_term = jnp.einsum(
            "tbd,cbd->tbc", grad_pre, layer_weights[:BLK], preferred_element_type=jnp.float32
        )
        if stride < blocks_dev or factor < FACTORS - 1 or bit_index - device_bits != 1:
            far_term = jnp.einsum(
                "tbd,cbd->tbc", grad_pre, layer_weights[BLK:], preferred_element_type=jnp.float32
            )
        if stride < blocks_dev:
            arrived = local_partner(far_term, stride)
        elif factor < FACTORS - 1 or bit_index - device_bits != 1:
            arrived = swapped(far_term, "tensor", bit_index - device_bits)
        else:
            arrived = jnp.einsum(
                "tbd,cbd->tbc",
                swapped(grad_pre, "tensor", 1),
                partner_rows(layer_weights[BLK:]),
                preferred_element_type=jnp.float32,
            )
        grad_hidden = near_term + arrived
        if factor > 0:
            previous = stored_preact[factor - 1]
            grad_pre = (grad_hidden * gelu_slope(previous)).astype(jnp.bfloat16)
    flat = grad_hidden.reshape(tok_rows, local_width)
    inner_sum = tensor_sum(jnp.sum(flat * normed, axis=1))
    token_grads = (
        cotangent.astype(jnp.float32) + inv_rms * (flat - normed * (inner_sum / D)[:, None])
    ).astype(jnp.bfloat16)
    weight_grads = scatter_rest(grad_terms[::-1])
    return (mixed, token_grads, weight_grads)


def solution(mesh):
    ny, nz, nx = 4, 4, 4
    fine = Mesh(
        mesh.devices.reshape(ny, nz, nx, mesh.shape["tensor"]), ("dy", "dz", "dx", "tensor")
    )
    dp = ("dy", "dz", "dx")
    return jax.shard_map(
        shards,
        mesh=fine,
        in_specs=(P(dp, "tensor"), P(None, None, "tensor", None), P(dp, "tensor")),
        out_specs=(P(dp, "tensor"), P(dp, "tensor"), P(None, dp, "tensor", None)),
        check_vma=False,
    )
```

```python
import math

import jax
import jax.numpy as jnp
from jax import lax
from jax.sharding import Mesh, PartitionSpec as P

D = 8192
BLK = 256
FACTORS = 3


root_half = 0.7071067811865476
pdf_scale = 0.3989422804014327
epsilon = 1e-06


def swapped(x, axis, stride):
    return lax.ppermute(x, axis, [(i, i ^ 1 << stride) for i in range(lax.axis_size(axis))])


def tensor_sum(x):
    for bit in range(lax.axis_size("tensor").bit_length() - 1):
        x = x + swapped(x, "tensor", bit)
    return x


def ring_scatter(x, axis):
    n = lax.axis_size(axis)
    me = lax.axis_index(axis)
    half = x.shape[1] // 2
    ways = ((x[:, :half], 1), (x[:, half:], n - 1))
    out = []
    for part, step in ways:
        acc = lax.dynamic_index_in_dim(part, (me + n - step) % n, 0, keepdims=False)
        for s in range(n - 1):
            recv = lax.ppermute(acc, axis, [(i, (i + step) % n) for i in range(n)])
            src = (me + n * (n + 1) - step * (s + 2)) % n
            acc = recv + lax.dynamic_index_in_dim(part, src, 0, keepdims=False)
        out.append(acc)
    return jnp.concatenate(out, axis=0)


def scatter_xy(grads):
    rows, blocks, lanes = grads.shape
    ny, nz, nx = (lax.axis_size(a) for a in ("dy", "dz", "dx"))
    share = rows // (ny * nz * nx)
    g = grads.reshape(ny, nz, nx, share, blocks, lanes)
    hb = blocks // 2
    gx = jnp.transpose(g[:, :, :, :, :hb], (2, 0, 1, 3, 4, 5))
    gy = jnp.transpose(g[:, :, :, :, hb:], (0, 2, 1, 3, 4, 5))
    gx = ring_scatter(ring_scatter(gx, "dx"), "dy")
    gy = ring_scatter(ring_scatter(gy, "dy"), "dx")
    return jnp.concatenate([gx, gy], axis=2)


def scatter_z(parts):
    nz, share, blocks, lanes = parts[0].shape
    g = jnp.stack(parts, axis=1).reshape(nz, -1, lanes)
    g = lax.psum_scatter(g, "dz", scatter_dimension=0, tiled=True)
    return g.reshape(len(parts), share, blocks, lanes)


def partner_rows(rows):
    pieces = lax.axis_size(("dy", "dx"))
    piece = rows.shape[0] // pieces
    mine = lax.axis_index("dy") * lax.axis_size("dx") + lax.axis_index("dx")
    part = lax.dynamic_slice_in_dim(rows, mine * piece, piece, axis=0)
    part = swapped(part, "tensor", 1)
    return lax.all_gather(part, ("dy", "dx"), axis=0, tiled=True)


def gelu_value(value):
    return value * (0.5 * (1.0 + lax.erf(value * root_half)))


def gelu_slope(value):
    return (
        0.5 * (1.0 + lax.erf(value * root_half)) + value * jnp.exp(-0.5 * value * value) * pdf_scale
    )


def local_partner(blocks, stride):
    tok_rows, block_count, width = blocks.shape
    folded = blocks.reshape(tok_rows, block_count // (2 * stride), 2, stride, width)
    return jnp.flip(folded, axis=2).reshape(tok_rows, block_count, width)


def apply_factor(hidden, partner, layer_weights):
    preact = jnp.einsum(
        "tbc,cbd->tbd", hidden, layer_weights[:BLK], preferred_element_type=jnp.float32
    )
    return preact + jnp.einsum(
        "tbc,cbd->tbd", partner, layer_weights[BLK:], preferred_element_type=jnp.float32
    )


def shards(tokens, weights, cotangent):
    tok_rows, local_width = tokens.shape
    blocks_dev = local_width // BLK
    block_bits = (D // BLK).bit_length() - 1
    device_bits = blocks_dev.bit_length() - 1
    data_size = lax.axis_size(("dy", "dz", "dx"))
    grad_scale = 1.0 / math.sqrt(tok_rows * data_size)
    tokens_f32 = tokens.astype(jnp.float32)
    square_sum = tensor_sum(jnp.sum(tokens_f32 * tokens_f32, axis=1))
    inv_rms = lax.rsqrt(square_sum / D + epsilon)[:, None]
    normed = tokens_f32 * inv_rms
    hidden = normed.astype(jnp.bfloat16).reshape(tok_rows, blocks_dev, BLK)
    stored_inputs = []
    stored_preact = []
    preact = None
    for factor in range(FACTORS):
        bit_index = block_bits - FACTORS + factor
        stride = 1 << bit_index
        if stride < blocks_dev:
            partner = local_partner(hidden, stride)
        else:
            partner = swapped(hidden, "tensor", bit_index - device_bits)
        preact = apply_factor(hidden, partner, weights[factor])
        stored_inputs.append((hidden, partner))
        stored_preact.append(preact)
        if factor < FACTORS - 1:
            hidden = gelu_value(preact).astype(jnp.bfloat16)
    mixed = (tokens_f32 + preact.reshape(tok_rows, local_width)).astype(jnp.bfloat16)
    grad_pre = cotangent.reshape(tok_rows, blocks_dev, BLK)
    grad_terms = []
    grad_hidden = None
    for factor in reversed(range(FACTORS)):
        bit_index = block_bits - FACTORS + factor
        stride = 1 << bit_index
        kept_hidden, kept_partner = stored_inputs[factor]
        joined = jnp.concatenate([kept_hidden, kept_partner], axis=2)
        grad_terms.append(
            scatter_xy(
                jnp.einsum("tbc,tbd->cbd", joined, grad_pre, preferred_element_type=jnp.float32)
                * grad_scale
            )
        )
        layer_weights = weights[factor]
        near_term = jnp.einsum(
            "tbd,cbd->tbc", grad_pre, layer_weights[:BLK], preferred_element_type=jnp.float32
        )
        if stride < blocks_dev or factor < FACTORS - 1 or bit_index - device_bits != 1:
            far_term = jnp.einsum(
                "tbd,cbd->tbc", grad_pre, layer_weights[BLK:], preferred_element_type=jnp.float32
            )
        if stride < blocks_dev:
            arrived = local_partner(far_term, stride)
        elif factor < FACTORS - 1 or bit_index - device_bits != 1:
            arrived = swapped(far_term, "tensor", bit_index - device_bits)
        else:
            arrived = jnp.einsum(
                "tbd,cbd->tbc",
                swapped(grad_pre, "tensor", 1),
                partner_rows(layer_weights[BLK:]),
                preferred_element_type=jnp.float32,
            )
        grad_hidden = near_term + arrived
        if factor > 0:
            previous = stored_preact[factor - 1]
            grad_pre = (grad_hidden * gelu_slope(previous)).astype(jnp.bfloat16)
    flat = grad_hidden.reshape(tok_rows, local_width)
    inner_sum = tensor_sum(jnp.sum(flat * normed, axis=1))
    token_grads = (
        cotangent.astype(jnp.float32) + inv_rms * (flat - normed * (inner_sum / D)[:, None])
    ).astype(jnp.bfloat16)
    weight_grads = scatter_z(grad_terms[::-1])
    return (mixed, token_grads, weight_grads)


def solution(mesh):
    ny, nz, nx = 4, 4, 4
    fine = Mesh(
        mesh.devices.reshape(ny, nz, nx, mesh.shape["tensor"]), ("dy", "dz", "dx", "tensor")
    )
    dp = ("dy", "dz", "dx")
    return jax.shard_map(
        shards,
        mesh=fine,
        in_specs=(P(dp, "tensor"), P(None, None, "tensor", None), P(dp, "tensor")),
        out_specs=(P(dp, "tensor"), P(dp, "tensor"), P(None, dp, "tensor", None)),
        check_vma=False,
    )
```

```python
import math

import jax
import jax.numpy as jnp
from jax import lax
from jax.sharding import Mesh, PartitionSpec as P

D = 8192
BLK = 256
FACTORS = 3


root_half = 0.7071067811865476
pdf_scale = 0.3989422804014327
epsilon = 1e-06


def swapped(x, axis, stride):
    return lax.ppermute(x, axis, [(i, i ^ 1 << stride) for i in range(lax.axis_size(axis))])


def tensor_sum(x):
    for bit in range(lax.axis_size("tensor").bit_length() - 1):
        x = x + swapped(x, "tensor", bit)
    return x


def dp_split(grads):
    rows, blocks, lanes = grads.shape
    ny, nz, nx = (lax.axis_size(a) for a in ("dy", "dz", "dx"))
    g = grads.reshape(ny, nz, nx, rows // (ny * nz * nx), blocks, lanes)
    return g[:, :, :, :, : blocks // 2], g[:, :, :, :, blocks // 2 :]


def scatter_x_first(half):
    g = jnp.moveaxis(half, 2, 0)
    shape = g.shape[1:]
    g = lax.psum_scatter(g.reshape(g.shape[0], -1, g.shape[-1]), "dx", scatter_dimension=0, tiled=True)
    return g.reshape(shape)


def exchange_sum(g, axis):
    return jnp.sum(lax.all_to_all(g, axis, 0, 0), axis=0)


def scatter_rest(x_parts, y_parts):
    ny = x_parts[0].shape[0]
    a = jnp.stack(x_parts, axis=1)
    shape = a.shape[1:]
    a = lax.psum_scatter(a.reshape(ny, -1, a.shape[-1]), "dy", scatter_dimension=0, tiled=True)
    a = a.reshape(shape)
    b = exchange_sum(jnp.stack(y_parts, axis=1), "dy")
    b = exchange_sum(jnp.moveaxis(b, 2, 0), "dx")
    g = jnp.concatenate([a, b], axis=-2)
    return exchange_sum(jnp.moveaxis(g, 1, 0), "dz")


def partner_rows(rows):
    pieces = lax.axis_size(("dy", "dx"))
    piece = rows.shape[0] // pieces
    mine = lax.axis_index("dy") * lax.axis_size("dx") + lax.axis_index("dx")
    part = lax.dynamic_slice_in_dim(rows, mine * piece, piece, axis=0)
    part = swapped(part, "tensor", 1)
    return lax.all_gather(part, ("dy", "dx"), axis=0, tiled=True)


def gelu_value(value):
    return value * (0.5 * (1.0 + lax.erf(value * root_half)))


def gelu_slope(value):
    return (
        0.5 * (1.0 + lax.erf(value * root_half)) + value * jnp.exp(-0.5 * value * value) * pdf_scale
    )


def local_partner(blocks, stride):
    tok_rows, block_count, width = blocks.shape
    folded = blocks.reshape(tok_rows, block_count // (2 * stride), 2, stride, width)
    return jnp.flip(folded, axis=2).reshape(tok_rows, block_count, width)


def apply_factor(hidden, partner, layer_weights):
    preact = jnp.einsum(
        "tbc,cbd->tbd", hidden, layer_weights[:BLK], preferred_element_type=jnp.float32
    )
    return preact + jnp.einsum(
        "tbc,cbd->tbd", partner, layer_weights[BLK:], preferred_element_type=jnp.float32
    )


def shards(tokens, weights, cotangent):
    tok_rows, local_width = tokens.shape
    blocks_dev = local_width // BLK
    block_bits = (D // BLK).bit_length() - 1
    device_bits = blocks_dev.bit_length() - 1
    data_size = lax.axis_size(("dy", "dz", "dx"))
    grad_scale = 1.0 / math.sqrt(tok_rows * data_size)
    tokens_f32 = tokens.astype(jnp.float32)
    square_sum = tensor_sum(jnp.sum(tokens_f32 * tokens_f32, axis=1))
    inv_rms = lax.rsqrt(square_sum / D + epsilon)[:, None]
    normed = tokens_f32 * inv_rms
    hidden = normed.astype(jnp.bfloat16).reshape(tok_rows, blocks_dev, BLK)
    stored_inputs = []
    stored_preact = []
    preact = None
    for factor in range(FACTORS):
        bit_index = block_bits - FACTORS + factor
        stride = 1 << bit_index
        if stride < blocks_dev:
            partner = local_partner(hidden, stride)
        else:
            partner = swapped(hidden, "tensor", bit_index - device_bits)
        preact = apply_factor(hidden, partner, weights[factor])
        stored_inputs.append((hidden, partner))
        stored_preact.append(preact)
        if factor < FACTORS - 1:
            hidden = gelu_value(preact).astype(jnp.bfloat16)
    mixed = (tokens_f32 + preact.reshape(tok_rows, local_width)).astype(jnp.bfloat16)
    grad_pre = cotangent.reshape(tok_rows, blocks_dev, BLK)
    grad_terms = []
    y_terms = []
    grad_hidden = None
    for factor in reversed(range(FACTORS)):
        bit_index = block_bits - FACTORS + factor
        stride = 1 << bit_index
        kept_hidden, kept_partner = stored_inputs[factor]
        joined = jnp.concatenate([kept_hidden, kept_partner], axis=2)
        x_half, y_half = dp_split(
            jnp.einsum("tbc,tbd->cbd", joined, grad_pre, preferred_element_type=jnp.float32)
            * grad_scale
        )
        grad_terms.append(scatter_x_first(x_half))
        y_terms.append(y_half)
        layer_weights = weights[factor]
        near_term = jnp.einsum(
            "tbd,cbd->tbc", grad_pre, layer_weights[:BLK], preferred_element_type=jnp.float32
        )
        if stride < blocks_dev or factor < FACTORS - 1 or bit_index - device_bits != 1:
            far_term = jnp.einsum(
                "tbd,cbd->tbc", grad_pre, layer_weights[BLK:], preferred_element_type=jnp.float32
            )
        if stride < blocks_dev:
            arrived = local_partner(far_term, stride)
        elif factor < FACTORS - 1 or bit_index - device_bits != 1:
            arrived = swapped(far_term, "tensor", bit_index - device_bits)
        else:
            arrived = jnp.einsum(
                "tbd,cbd->tbc",
                swapped(grad_pre, "tensor", 1),
                partner_rows(layer_weights[BLK:]),
                preferred_element_type=jnp.float32,
            )
        grad_hidden = near_term + arrived
        if factor > 0:
            previous = stored_preact[factor - 1]
            grad_pre = (grad_hidden * gelu_slope(previous)).astype(jnp.bfloat16)
    flat = grad_hidden.reshape(tok_rows, local_width)
    inner_sum = tensor_sum(jnp.sum(flat * normed, axis=1))
    token_grads = (
        cotangent.astype(jnp.float32) + inv_rms * (flat - normed * (inner_sum / D)[:, None])
    ).astype(jnp.bfloat16)
    weight_grads = scatter_rest(grad_terms[::-1], y_terms[::-1])
    return (mixed, token_grads, weight_grads)


def solution(mesh):
    ny, nz, nx = 4, 4, 4
    fine = Mesh(
        mesh.devices.reshape(ny, nz, nx, mesh.shape["tensor"]), ("dy", "dz", "dx", "tensor")
    )
    dp = ("dy", "dz", "dx")
    return jax.shard_map(
        shards,
        mesh=fine,
        in_specs=(P(dp, "tensor"), P(None, None, "tensor", None), P(dp, "tensor")),
        out_specs=(P(dp, "tensor"), P(dp, "tensor"), P(None, dp, "tensor", None)),
        check_vma=False,
    )
```

```python
import math

import jax
import jax.numpy as jnp
from jax import lax
from jax.sharding import Mesh, PartitionSpec as P

D = 8192
BLK = 256
FACTORS = 3


root_half = 0.7071067811865476
pdf_scale = 0.3989422804014327
epsilon = 1e-06


def swapped(x, axis, stride):
    return lax.ppermute(x, axis, [(i, i ^ 1 << stride) for i in range(lax.axis_size(axis))])


def tensor_sum(x):
    for bit in range(lax.axis_size("tensor").bit_length() - 1):
        x = x + swapped(x, "tensor", bit)
    return x


def scatter_first(grads):
    rows = grads.shape[0]
    ny, nz, nx = (lax.axis_size(a) for a in ("dy", "dz", "dx"))
    rest = grads.shape[1:]
    share = rows // (ny * nz * nx)
    g = grads.reshape((ny, nz, nx, share) + rest)
    g = jnp.moveaxis(g, 2, 0).reshape(nx, -1, rest[-1])
    g = lax.psum_scatter(g, "dx", scatter_dimension=0, tiled=True)
    return g.reshape((ny, nz, share) + rest)


def scatter_rest(parts):
    ny, nz, share = parts[0].shape[:3]
    rest = parts[0].shape[3:]
    g = jnp.stack(parts, axis=2)
    for axis, size in (("dy", ny), ("dz", nz)):
        g = g.reshape(size, -1, rest[-1])
        g = lax.psum_scatter(g, axis, scatter_dimension=0, tiled=True)
    return g.reshape((len(parts), share) + rest)


def partner_rows(rows):
    pieces = lax.axis_size(("dy", "dx"))
    piece = rows.shape[0] // pieces
    mine = lax.axis_index("dy") * lax.axis_size("dx") + lax.axis_index("dx")
    part = lax.dynamic_slice_in_dim(rows, mine * piece, piece, axis=0)
    part = swapped(part, "tensor", 1)
    return lax.all_gather(part, ("dy", "dx"), axis=0, tiled=True)


def gelu_value(value):
    return value * (0.5 * (1.0 + lax.erf(value * root_half)))


def gelu_slope(value):
    return (
        0.5 * (1.0 + lax.erf(value * root_half)) + value * jnp.exp(-0.5 * value * value) * pdf_scale
    )


def local_partner(blocks, stride):
    tok_rows, block_count, width = blocks.shape
    folded = blocks.reshape(tok_rows, block_count // (2 * stride), 2, stride, width)
    return jnp.flip(folded, axis=2).reshape(tok_rows, block_count, width)


def apply_factor(hidden, partner, layer_weights):
    preact = jnp.einsum(
        "tbc,cbd->tbd", hidden, layer_weights[:BLK], preferred_element_type=jnp.float32
    )
    return preact + jnp.einsum(
        "tbc,cbd->tbd", partner, layer_weights[BLK:], preferred_element_type=jnp.float32
    )


def shards(tokens, weights, cotangent):
    tok_rows, local_width = tokens.shape
    blocks_dev = local_width // BLK
    block_bits = (D // BLK).bit_length() - 1
    device_bits = blocks_dev.bit_length() - 1
    data_size = lax.axis_size(("dy", "dz", "dx"))
    grad_scale = 1.0 / math.sqrt(tok_rows * data_size)
    top = FACTORS - 1
    assert block_bits - 1 - device_bits == 1
    cot_blocks = cotangent.reshape(tok_rows, blocks_dev, BLK)
    partner_cot = swapped(cot_blocks, "tensor", 1)
    tokens_f32 = tokens.astype(jnp.float32)
    square_sum = tensor_sum(jnp.sum(tokens_f32 * tokens_f32, axis=1))
    inv_rms = lax.rsqrt(square_sum / D + epsilon)[:, None]
    normed = tokens_f32 * inv_rms
    hidden = normed.astype(jnp.bfloat16).reshape(tok_rows, blocks_dev, BLK)
    stored_inputs = []
    stored_preact = []
    for factor in range(top):
        bit_index = block_bits - FACTORS + factor
        stride = 1 << bit_index
        if stride < blocks_dev:
            partner = local_partner(hidden, stride)
        else:
            partner = swapped(hidden, "tensor", bit_index - device_bits)
        preact = apply_factor(hidden, partner, weights[factor])
        stored_inputs.append((hidden, partner))
        stored_preact.append(preact)
        hidden = gelu_value(preact).astype(jnp.bfloat16)
    hidden, partner_cot = lax.optimization_barrier((hidden, partner_cot))
    partner_top = swapped(hidden, "tensor", 1)
    top_weights = weights[top]
    grad_hidden = jnp.einsum(
        "tbd,cbd->tbc", cot_blocks, top_weights[:BLK], preferred_element_type=jnp.float32
    ) + jnp.einsum(
        "tbd,cbd->tbc",
        partner_cot,
        partner_rows(top_weights[BLK:]),
        preferred_element_type=jnp.float32,
    )
    grad_pre = (grad_hidden * gelu_slope(stored_preact[top - 1])).astype(jnp.bfloat16)
    grad_terms = [None] * FACTORS
    for factor in reversed(range(top)):
        bit_index = block_bits - FACTORS + factor
        stride = 1 << bit_index
        kept_hidden, kept_partner = stored_inputs[factor]
        joined = jnp.concatenate([kept_hidden, kept_partner], axis=2)
        grad_terms[factor] = scatter_first(
            jnp.einsum("tbc,tbd->cbd", joined, grad_pre, preferred_element_type=jnp.float32)
            * grad_scale
        )
        layer_weights = weights[factor]
        near_term = jnp.einsum(
            "tbd,cbd->tbc", grad_pre, layer_weights[:BLK], preferred_element_type=jnp.float32
        )
        far_term = jnp.einsum(
            "tbd,cbd->tbc", grad_pre, layer_weights[BLK:], preferred_element_type=jnp.float32
        )
        if stride < blocks_dev:
            arrived = local_partner(far_term, stride)
        else:
            arrived = swapped(far_term, "tensor", bit_index - device_bits)
        grad_hidden = near_term + arrived
        if factor > 0:
            previous = stored_preact[factor - 1]
            grad_pre = (grad_hidden * gelu_slope(previous)).astype(jnp.bfloat16)
    partner_top, _ = lax.optimization_barrier((partner_top, grad_hidden))
    preact = apply_factor(hidden, partner_top, top_weights)
    mixed = (tokens_f32 + preact.reshape(tok_rows, local_width)).astype(jnp.bfloat16)
    joined = jnp.concatenate([hidden, partner_top], axis=2)
    grad_terms[top] = scatter_first(
        jnp.einsum("tbc,tbd->cbd", joined, cot_blocks, preferred_element_type=jnp.float32)
        * grad_scale
    )
    flat = grad_hidden.reshape(tok_rows, local_width)
    inner_sum = tensor_sum(jnp.sum(flat * normed, axis=1))
    token_grads = (
        cotangent.astype(jnp.float32) + inv_rms * (flat - normed * (inner_sum / D)[:, None])
    ).astype(jnp.bfloat16)
    weight_grads = scatter_rest(grad_terms)
    return (mixed, token_grads, weight_grads)


def solution(mesh):
    ny, nz, nx = 4, 4, 4
    fine = Mesh(
        mesh.devices.reshape(ny, nz, nx, mesh.shape["tensor"]), ("dy", "dz", "dx", "tensor")
    )
    dp = ("dy", "dz", "dx")
    return jax.shard_map(
        shards,
        mesh=fine,
        in_specs=(P(dp, "tensor"), P(None, None, "tensor", None), P(dp, "tensor")),
        out_specs=(P(dp, "tensor"), P(dp, "tensor"), P(None, dp, "tensor", None)),
        check_vma=False,
    )
```

```python
import math

import jax
import jax.numpy as jnp
from jax import lax
from jax.sharding import Mesh, PartitionSpec as P

D = 8192
BLK = 256
FACTORS = 3


root_half = 0.7071067811865476
pdf_scale = 0.3989422804014327
epsilon = 1e-06


def swapped(x, axis, stride):
    return lax.ppermute(x, axis, [(i, i ^ 1 << stride) for i in range(lax.axis_size(axis))])


def tensor_sum(x):
    for bit in range(lax.axis_size("tensor").bit_length() - 1):
        x = x + swapped(x, "tensor", bit)
    return x


def scatter_first(grads):
    rows = grads.shape[0]
    ny, nz, nx = (lax.axis_size(a) for a in ("dy", "dz", "dx"))
    rest = grads.shape[1:]
    share = rows // (ny * nz * nx)
    g = grads.reshape((ny, nz, nx, share) + rest)
    g = jnp.moveaxis(g, 2, 0).reshape(nx, -1, rest[-1])
    g = lax.psum_scatter(g, "dx", scatter_dimension=0, tiled=True)
    return g.reshape((ny, nz, share) + rest)


def exchange_sum(g, axis):
    return jnp.sum(lax.all_to_all(g, axis, 0, 0), axis=0)


def scatter_by_exchange(grads):
    rows = grads.shape[0]
    rest = grads.shape[1:]
    ny, nz, nx = (lax.axis_size(a) for a in ("dy", "dz", "dx"))
    g = grads.reshape((ny, nz, nx, rows // (ny * nz * nx)) + rest)
    g = exchange_sum(g, "dy")
    return exchange_sum(jnp.moveaxis(g, 1, 0), "dx")


def scatter_rest(sc_parts, tc_parts):
    ny, nz = sc_parts[0].shape[:2]
    g = jnp.stack(sc_parts, axis=1)
    shape = g.shape[1:]
    g = lax.psum_scatter(g.reshape(ny, -1, g.shape[-1]), "dy", scatter_dimension=0, tiled=True)
    g = jnp.concatenate([g.reshape(shape), jnp.stack(tc_parts, axis=0)], axis=0)
    return exchange_sum(jnp.moveaxis(g, 1, 0), "dz")


def partner_rows(rows):
    pieces = lax.axis_size(("dy", "dx"))
    piece = rows.shape[0] // pieces
    mine = lax.axis_index("dy") * lax.axis_size("dx") + lax.axis_index("dx")
    part = lax.dynamic_slice_in_dim(rows, mine * piece, piece, axis=0)
    part = swapped(part, "tensor", 1)
    return lax.all_gather(part, ("dy", "dx"), axis=0, tiled=True)


def gelu_value(value):
    return value * (0.5 * (1.0 + lax.erf(value * root_half)))


def gelu_slope(value):
    return (
        0.5 * (1.0 + lax.erf(value * root_half)) + value * jnp.exp(-0.5 * value * value) * pdf_scale
    )


def local_partner(blocks, stride):
    tok_rows, block_count, width = blocks.shape
    folded = blocks.reshape(tok_rows, block_count // (2 * stride), 2, stride, width)
    return jnp.flip(folded, axis=2).reshape(tok_rows, block_count, width)


def apply_factor(hidden, partner, layer_weights):
    preact = jnp.einsum(
        "tbc,cbd->tbd", hidden, layer_weights[:BLK], preferred_element_type=jnp.float32
    )
    return preact + jnp.einsum(
        "tbc,cbd->tbd", partner, layer_weights[BLK:], preferred_element_type=jnp.float32
    )


def shards(tokens, weights, cotangent):
    tok_rows, local_width = tokens.shape
    blocks_dev = local_width // BLK
    block_bits = (D // BLK).bit_length() - 1
    device_bits = blocks_dev.bit_length() - 1
    data_size = lax.axis_size(("dy", "dz", "dx"))
    grad_scale = 1.0 / math.sqrt(tok_rows * data_size)
    top = FACTORS - 1
    assert block_bits - 1 - device_bits == 1
    cot_blocks = cotangent.reshape(tok_rows, blocks_dev, BLK)
    partner_cot = swapped(cot_blocks, "tensor", 1)
    tokens_f32 = tokens.astype(jnp.float32)
    square_sum = tensor_sum(jnp.sum(tokens_f32 * tokens_f32, axis=1))
    inv_rms = lax.rsqrt(square_sum / D + epsilon)[:, None]
    normed = tokens_f32 * inv_rms
    hidden = normed.astype(jnp.bfloat16).reshape(tok_rows, blocks_dev, BLK)
    stored_inputs = []
    stored_preact = []
    for factor in range(top):
        bit_index = block_bits - FACTORS + factor
        stride = 1 << bit_index
        if stride < blocks_dev:
            partner = local_partner(hidden, stride)
        else:
            partner = swapped(hidden, "tensor", bit_index - device_bits)
        preact = apply_factor(hidden, partner, weights[factor])
        stored_inputs.append((hidden, partner))
        stored_preact.append(preact)
        hidden = gelu_value(preact).astype(jnp.bfloat16)
    hidden, partner_cot = lax.optimization_barrier((hidden, partner_cot))
    partner_top = swapped(hidden, "tensor", 1)
    top_weights = weights[top]
    grad_hidden = jnp.einsum(
        "tbd,cbd->tbc", cot_blocks, top_weights[:BLK], preferred_element_type=jnp.float32
    ) + jnp.einsum(
        "tbd,cbd->tbc",
        partner_cot,
        partner_rows(top_weights[BLK:]),
        preferred_element_type=jnp.float32,
    )
    grad_pre = (grad_hidden * gelu_slope(stored_preact[top - 1])).astype(jnp.bfloat16)
    grad_terms = [None] * FACTORS
    for factor in reversed(range(top)):
        bit_index = block_bits - FACTORS + factor
        stride = 1 << bit_index
        kept_hidden, kept_partner = stored_inputs[factor]
        joined = jnp.concatenate([kept_hidden, kept_partner], axis=2)
        grad_terms[factor] = scatter_first(
            jnp.einsum("tbc,tbd->cbd", joined, grad_pre, preferred_element_type=jnp.float32)
            * grad_scale
        )
        layer_weights = weights[factor]
        near_term = jnp.einsum(
            "tbd,cbd->tbc", grad_pre, layer_weights[:BLK], preferred_element_type=jnp.float32
        )
        far_term = jnp.einsum(
            "tbd,cbd->tbc", grad_pre, layer_weights[BLK:], preferred_element_type=jnp.float32
        )
        if stride < blocks_dev:
            arrived = local_partner(far_term, stride)
        else:
            arrived = swapped(far_term, "tensor", bit_index - device_bits)
        grad_hidden = near_term + arrived
        if factor > 0:
            previous = stored_preact[factor - 1]
            grad_pre = (grad_hidden * gelu_slope(previous)).astype(jnp.bfloat16)
    partner_top, _ = lax.optimization_barrier((partner_top, grad_hidden))
    preact = apply_factor(hidden, partner_top, top_weights)
    mixed = (tokens_f32 + preact.reshape(tok_rows, local_width)).astype(jnp.bfloat16)
    joined = jnp.concatenate([hidden, partner_top], axis=2)
    top_term = scatter_by_exchange(
        jnp.einsum("tbc,tbd->cbd", joined, cot_blocks, preferred_element_type=jnp.float32)
        * grad_scale
    )
    flat = grad_hidden.reshape(tok_rows, local_width)
    inner_sum = tensor_sum(jnp.sum(flat * normed, axis=1))
    token_grads = (
        cotangent.astype(jnp.float32) + inv_rms * (flat - normed * (inner_sum / D)[:, None])
    ).astype(jnp.bfloat16)
    weight_grads = scatter_rest(grad_terms[:top], [top_term])
    return (mixed, token_grads, weight_grads)


def solution(mesh):
    ny, nz, nx = 4, 4, 4
    fine = Mesh(
        mesh.devices.reshape(ny, nz, nx, mesh.shape["tensor"]), ("dy", "dz", "dx", "tensor")
    )
    dp = ("dy", "dz", "dx")
    return jax.shard_map(
        shards,
        mesh=fine,
        in_specs=(P(dp, "tensor"), P(None, None, "tensor", None), P(dp, "tensor")),
        out_specs=(P(dp, "tensor"), P(dp, "tensor"), P(None, dp, "tensor", None)),
        check_vma=False,
    )
```

```python
import math

import jax
import jax.numpy as jnp
from jax import lax
from jax.sharding import Mesh, PartitionSpec as P

D = 8192
BLK = 256
FACTORS = 3


root_half = 0.7071067811865476
pdf_scale = 0.3989422804014327
epsilon = 1e-06


def swapped(x, axis, stride):
    return lax.ppermute(x, axis, [(i, i ^ 1 << stride) for i in range(lax.axis_size(axis))])


def tensor_sum(x):
    for bit in range(lax.axis_size("tensor").bit_length() - 1):
        x = x + swapped(x, "tensor", bit)
    return x


def exchange_sum(g, axis):
    return jnp.sum(lax.all_to_all(g, axis, 0, 0), axis=0)


def scatter_lead(g, axis):
    shape = g.shape[1:]
    g = lax.psum_scatter(g.reshape(g.shape[0], -1, g.shape[-1]), axis, scatter_dimension=0, tiled=True)
    return g.reshape(shape)


def scatter_dp(terms):
    rows, blocks, lanes = terms[0].shape
    ny, nz, nx = (lax.axis_size(a) for a in ("dy", "dz", "dx"))
    share = rows // (ny * nz * nx)
    g = jnp.stack(terms, axis=0).reshape(len(terms), ny, nz, nx, share, blocks, lanes)
    hb = blocks // 2
    on_sc = jnp.moveaxis(g[..., :hb, :], 1, 0)
    on_tc = jnp.moveaxis(g[..., hb:, :], 3, 0)
    on_sc = scatter_lead(on_sc, "dy")
    on_tc = exchange_sum(on_tc, "dx")
    on_sc = scatter_lead(jnp.moveaxis(on_sc, 2, 0), "dx")
    on_tc = exchange_sum(jnp.moveaxis(on_tc, 1, 0), "dy")
    g = jnp.concatenate([on_sc, on_tc], axis=-2)
    return exchange_sum(jnp.moveaxis(g, 1, 0), "dz")


def partner_rows(rows):
    pieces = lax.axis_size(("dy", "dx"))
    piece = rows.shape[0] // pieces
    mine = lax.axis_index("dy") * lax.axis_size("dx") + lax.axis_index("dx")
    part = lax.dynamic_slice_in_dim(rows, mine * piece, piece, axis=0)
    part = swapped(part, "tensor", 1)
    return lax.all_gather(part, ("dy", "dx"), axis=0, tiled=True)


def gelu_value(value):
    return value * (0.5 * (1.0 + lax.erf(value * root_half)))


def gelu_slope(value):
    return (
        0.5 * (1.0 + lax.erf(value * root_half)) + value * jnp.exp(-0.5 * value * value) * pdf_scale
    )


def local_partner(blocks, stride):
    tok_rows, block_count, width = blocks.shape
    folded = blocks.reshape(tok_rows, block_count // (2 * stride), 2, stride, width)
    return jnp.flip(folded, axis=2).reshape(tok_rows, block_count, width)


def apply_factor(hidden, partner, layer_weights):
    preact = jnp.einsum(
        "tbc,cbd->tbd", hidden, layer_weights[:BLK], preferred_element_type=jnp.float32
    )
    return preact + jnp.einsum(
        "tbc,cbd->tbd", partner, layer_weights[BLK:], preferred_element_type=jnp.float32
    )


def shards(tokens, weights, cotangent):
    tok_rows, local_width = tokens.shape
    blocks_dev = local_width // BLK
    block_bits = (D // BLK).bit_length() - 1
    device_bits = blocks_dev.bit_length() - 1
    data_size = lax.axis_size(("dy", "dz", "dx"))
    grad_scale = 1.0 / math.sqrt(tok_rows * data_size)
    top = FACTORS - 1
    assert block_bits - 1 - device_bits == 1
    cot_blocks = cotangent.reshape(tok_rows, blocks_dev, BLK)
    partner_cot = swapped(cot_blocks, "tensor", 1)
    tokens_f32 = tokens.astype(jnp.float32)
    square_sum = tensor_sum(jnp.sum(tokens_f32 * tokens_f32, axis=1))
    inv_rms = lax.rsqrt(square_sum / D + epsilon)[:, None]
    normed = tokens_f32 * inv_rms
    hidden = normed.astype(jnp.bfloat16).reshape(tok_rows, blocks_dev, BLK)
    stored_inputs = []
    stored_preact = []
    for factor in range(top):
        bit_index = block_bits - FACTORS + factor
        stride = 1 << bit_index
        if stride < blocks_dev:
            partner = local_partner(hidden, stride)
        else:
            partner = swapped(hidden, "tensor", bit_index - device_bits)
        preact = apply_factor(hidden, partner, weights[factor])
        stored_inputs.append((hidden, partner))
        stored_preact.append(preact)
        hidden = gelu_value(preact).astype(jnp.bfloat16)
    hidden, partner_cot = lax.optimization_barrier((hidden, partner_cot))
    partner_top = swapped(hidden, "tensor", 1)
    top_weights = weights[top]
    grad_hidden = jnp.einsum(
        "tbd,cbd->tbc", cot_blocks, top_weights[:BLK], preferred_element_type=jnp.float32
    ) + jnp.einsum(
        "tbd,cbd->tbc",
        partner_cot,
        partner_rows(top_weights[BLK:]),
        preferred_element_type=jnp.float32,
    )
    grad_pre = (grad_hidden * gelu_slope(stored_preact[top - 1])).astype(jnp.bfloat16)
    grad_terms = [None] * FACTORS
    for factor in reversed(range(top)):
        bit_index = block_bits - FACTORS + factor
        stride = 1 << bit_index
        kept_hidden, kept_partner = stored_inputs[factor]
        joined = jnp.concatenate([kept_hidden, kept_partner], axis=2)
        grad_terms[factor] = (
            jnp.einsum("tbc,tbd->cbd", joined, grad_pre, preferred_element_type=jnp.float32)
            * grad_scale
        )
        layer_weights = weights[factor]
        near_term = jnp.einsum(
            "tbd,cbd->tbc", grad_pre, layer_weights[:BLK], preferred_element_type=jnp.float32
        )
        far_term = jnp.einsum(
            "tbd,cbd->tbc", grad_pre, layer_weights[BLK:], preferred_element_type=jnp.float32
        )
        if stride < blocks_dev:
            arrived = local_partner(far_term, stride)
        else:
            arrived = swapped(far_term, "tensor", bit_index - device_bits)
        grad_hidden = near_term + arrived
        if factor > 0:
            previous = stored_preact[factor - 1]
            grad_pre = (grad_hidden * gelu_slope(previous)).astype(jnp.bfloat16)
    partner_top, _ = lax.optimization_barrier((partner_top, grad_hidden))
    preact = apply_factor(hidden, partner_top, top_weights)
    mixed = (tokens_f32 + preact.reshape(tok_rows, local_width)).astype(jnp.bfloat16)
    joined = jnp.concatenate([hidden, partner_top], axis=2)
    grad_terms[top] = (
        jnp.einsum("tbc,tbd->cbd", joined, cot_blocks, preferred_element_type=jnp.float32)
        * grad_scale
    )
    flat = grad_hidden.reshape(tok_rows, local_width)
    inner_sum = tensor_sum(jnp.sum(flat * normed, axis=1))
    token_grads = (
        cotangent.astype(jnp.float32) + inv_rms * (flat - normed * (inner_sum / D)[:, None])
    ).astype(jnp.bfloat16)
    weight_grads = scatter_dp(grad_terms)
    return (mixed, token_grads, weight_grads)


def solution(mesh):
    ny, nz, nx = 4, 4, 4
    fine = Mesh(
        mesh.devices.reshape(ny, nz, nx, mesh.shape["tensor"]), ("dy", "dz", "dx", "tensor")
    )
    dp = ("dy", "dz", "dx")
    return jax.shard_map(
        shards,
        mesh=fine,
        in_specs=(P(dp, "tensor"), P(None, None, "tensor", None), P(dp, "tensor")),
        out_specs=(P(dp, "tensor"), P(dp, "tensor"), P(None, dp, "tensor", None)),
        check_vma=False,
    )
```

```python
import math

import jax
import jax.numpy as jnp
from jax import lax
from jax.sharding import Mesh, PartitionSpec as P

D = 8192
BLK = 256
FACTORS = 3


root_half = 0.7071067811865476
pdf_scale = 0.3989422804014327
epsilon = 1e-06


def swapped(x, axis, stride):
    return lax.ppermute(x, axis, [(i, i ^ 1 << stride) for i in range(lax.axis_size(axis))])


def tensor_sum(x):
    for bit in range(lax.axis_size("tensor").bit_length() - 1):
        x = x + swapped(x, "tensor", bit)
    return x


def scatter_first(grads):
    rows = grads.shape[0]
    ny, nz, nx = (lax.axis_size(a) for a in ("dy", "dz", "dx"))
    rest = grads.shape[1:]
    share = rows // (ny * nz * nx)
    g = lax.psum_scatter(grads.reshape(ny, -1, rest[-1]), "dy", scatter_dimension=0, tiled=True)
    return g.reshape((nz, nx, share) + rest)


def scatter_rest(parts):
    nz, nx, share = parts[0].shape[:3]
    rest = parts[0].shape[3:]
    g = jnp.moveaxis(jnp.stack(parts, axis=0), 2, 0)
    g = lax.psum_scatter(g.reshape(nx, -1, rest[-1]), "dx", scatter_dimension=0, tiled=True)
    g = jnp.moveaxis(g.reshape((len(parts), nz, share) + rest), 1, 0)
    g = lax.psum_scatter(g.reshape(nz, -1, rest[-1]), "dz", scatter_dimension=0, tiled=True)
    return g.reshape((len(parts), share) + rest)


def partner_rows(rows):
    pieces = lax.axis_size(("dy", "dx"))
    piece = rows.shape[0] // pieces
    mine = lax.axis_index("dy") * lax.axis_size("dx") + lax.axis_index("dx")
    part = lax.dynamic_slice_in_dim(rows, mine * piece, piece, axis=0)
    part = swapped(part, "tensor", 1)
    return lax.all_gather(part, ("dy", "dx"), axis=0, tiled=True)


def gelu_value(value):
    return value * (0.5 * (1.0 + lax.erf(value * root_half)))


def gelu_slope(value):
    return (
        0.5 * (1.0 + lax.erf(value * root_half)) + value * jnp.exp(-0.5 * value * value) * pdf_scale
    )


def local_partner(blocks, stride):
    tok_rows, block_count, width = blocks.shape
    folded = blocks.reshape(tok_rows, block_count // (2 * stride), 2, stride, width)
    return jnp.flip(folded, axis=2).reshape(tok_rows, block_count, width)


def apply_factor(hidden, partner, layer_weights):
    preact = jnp.einsum(
        "tbc,cbd->tbd", hidden, layer_weights[:BLK], preferred_element_type=jnp.float32
    )
    return preact + jnp.einsum(
        "tbc,cbd->tbd", partner, layer_weights[BLK:], preferred_element_type=jnp.float32
    )


def shards(tokens, weights, cotangent):
    tok_rows, local_width = tokens.shape
    blocks_dev = local_width // BLK
    block_bits = (D // BLK).bit_length() - 1
    device_bits = blocks_dev.bit_length() - 1
    data_size = lax.axis_size(("dy", "dz", "dx"))
    grad_scale = 1.0 / math.sqrt(tok_rows * data_size)
    top = FACTORS - 1
    assert block_bits - 1 - device_bits == 1
    cot_blocks = cotangent.reshape(tok_rows, blocks_dev, BLK)
    partner_cot = swapped(cot_blocks, "tensor", 1)
    tokens_f32 = tokens.astype(jnp.float32)
    square_sum = tensor_sum(jnp.sum(tokens_f32 * tokens_f32, axis=1))
    inv_rms = lax.rsqrt(square_sum / D + epsilon)[:, None]
    normed = tokens_f32 * inv_rms
    hidden = normed.astype(jnp.bfloat16).reshape(tok_rows, blocks_dev, BLK)
    stored_inputs = []
    stored_preact = []
    for factor in range(top):
        bit_index = block_bits - FACTORS + factor
        stride = 1 << bit_index
        if stride < blocks_dev:
            partner = local_partner(hidden, stride)
        else:
            partner = swapped(hidden, "tensor", bit_index - device_bits)
        preact = apply_factor(hidden, partner, weights[factor])
        stored_inputs.append((hidden, partner))
        stored_preact.append(preact)
        hidden = gelu_value(preact).astype(jnp.bfloat16)
    hidden, partner_cot = lax.optimization_barrier((hidden, partner_cot))
    partner_top = swapped(hidden, "tensor", 1)
    top_weights = weights[top]
    grad_hidden = jnp.einsum(
        "tbd,cbd->tbc", cot_blocks, top_weights[:BLK], preferred_element_type=jnp.float32
    ) + jnp.einsum(
        "tbd,cbd->tbc",
        partner_cot,
        partner_rows(top_weights[BLK:]),
        preferred_element_type=jnp.float32,
    )
    grad_pre = (grad_hidden * gelu_slope(stored_preact[top - 1])).astype(jnp.bfloat16)
    grad_terms = [None] * FACTORS
    for factor in reversed(range(top)):
        bit_index = block_bits - FACTORS + factor
        stride = 1 << bit_index
        kept_hidden, kept_partner = stored_inputs[factor]
        joined = jnp.concatenate([kept_hidden, kept_partner], axis=2)
        grad_terms[factor] = scatter_first(
            jnp.einsum("tbc,tbd->cbd", joined, grad_pre, preferred_element_type=jnp.float32)
            * grad_scale
        )
        layer_weights = weights[factor]
        near_term = jnp.einsum(
            "tbd,cbd->tbc", grad_pre, layer_weights[:BLK], preferred_element_type=jnp.float32
        )
        far_term = jnp.einsum(
            "tbd,cbd->tbc", grad_pre, layer_weights[BLK:], preferred_element_type=jnp.float32
        )
        if stride < blocks_dev:
            arrived = local_partner(far_term, stride)
        else:
            arrived = swapped(far_term, "tensor", bit_index - device_bits)
        grad_hidden = near_term + arrived
        if factor > 0:
            previous = stored_preact[factor - 1]
            grad_pre = (grad_hidden * gelu_slope(previous)).astype(jnp.bfloat16)
    partner_top, _ = lax.optimization_barrier((partner_top, grad_hidden))
    preact = apply_factor(hidden, partner_top, top_weights)
    mixed = (tokens_f32 + preact.reshape(tok_rows, local_width)).astype(jnp.bfloat16)
    joined = jnp.concatenate([hidden, partner_top], axis=2)
    grad_terms[top] = scatter_first(
        jnp.einsum("tbc,tbd->cbd", joined, cot_blocks, preferred_element_type=jnp.float32)
        * grad_scale
    )
    flat = grad_hidden.reshape(tok_rows, local_width)
    inner_sum = tensor_sum(jnp.sum(flat * normed, axis=1))
    token_grads = (
        cotangent.astype(jnp.float32) + inv_rms * (flat - normed * (inner_sum / D)[:, None])
    ).astype(jnp.bfloat16)
    weight_grads = scatter_rest(grad_terms)
    return (mixed, token_grads, weight_grads)


def solution(mesh):
    ny, nz, nx = 4, 4, 4
    fine = Mesh(
        mesh.devices.reshape(ny, nz, nx, mesh.shape["tensor"]), ("dy", "dz", "dx", "tensor")
    )
    dp = ("dy", "dz", "dx")
    return jax.shard_map(
        shards,
        mesh=fine,
        in_specs=(P(dp, "tensor"), P(None, None, "tensor", None), P(dp, "tensor")),
        out_specs=(P(dp, "tensor"), P(dp, "tensor"), P(None, dp, "tensor", None)),
        check_vma=False,
    )
```

```python
import math

import jax
import jax.numpy as jnp
from jax import lax
from jax.sharding import Mesh, PartitionSpec as P

D = 8192
BLK = 256
FACTORS = 3


root_half = 0.7071067811865476
pdf_scale = 0.3989422804014327
epsilon = 1e-06


def swapped(x, axis, stride):
    return lax.ppermute(x, axis, [(i, i ^ 1 << stride) for i in range(lax.axis_size(axis))])


def tensor_sum(x):
    for bit in range(lax.axis_size("tensor").bit_length() - 1):
        x = x + swapped(x, "tensor", bit)
    return x


def scatter_first(grads):
    rows = grads.shape[0]
    ny, nz, nx = (lax.axis_size(a) for a in ("dy", "dz", "dx"))
    rest = grads.shape[1:]
    share = rows // (ny * nz * nx)
    g = lax.psum_scatter(grads.reshape(ny, -1, rest[-1]), "dy", scatter_dimension=0, tiled=True)
    return g.reshape((nz, nx, share) + rest)


def exchange_first(grads):
    rows = grads.shape[0]
    ny, nz, nx = (lax.axis_size(a) for a in ("dy", "dz", "dx"))
    rest = grads.shape[1:]
    g = grads.reshape((ny, nz, nx, rows // (ny * nz * nx)) + rest)
    return jnp.sum(lax.all_to_all(g, "dx", 2, 2), axis=2)


def scatter_rest(on_sc, on_tc):
    nz, nx, share = on_sc[0].shape[:3]
    rest = on_sc[0].shape[3:]
    a, on_tc = lax.optimization_barrier((jnp.stack(on_sc, axis=0), on_tc))
    a = jnp.moveaxis(a, 2, 0)
    a = lax.psum_scatter(a.reshape(nx, -1, rest[-1]), "dx", scatter_dimension=0, tiled=True)
    a = a.reshape((len(on_sc), nz, share) + rest)
    b = jnp.sum(lax.all_to_all(on_tc, "dy", 0, 0), axis=0)
    g = jnp.moveaxis(jnp.concatenate([b[None], a], axis=0), 1, 0)
    g = lax.psum_scatter(g.reshape(nz, -1, rest[-1]), "dz", scatter_dimension=0, tiled=True)
    return g.reshape((len(on_sc) + 1, share) + rest)


def partner_rows(rows):
    pieces = lax.axis_size(("dy", "dx"))
    piece = rows.shape[0] // pieces
    mine = lax.axis_index("dy") * lax.axis_size("dx") + lax.axis_index("dx")
    part = lax.dynamic_slice_in_dim(rows, mine * piece, piece, axis=0)
    part = swapped(part, "tensor", 1)
    return lax.all_gather(part, ("dy", "dx"), axis=0, tiled=True)


def gelu_value(value):
    return value * (0.5 * (1.0 + lax.erf(value * root_half)))


def gelu_slope(value):
    return (
        0.5 * (1.0 + lax.erf(value * root_half)) + value * jnp.exp(-0.5 * value * value) * pdf_scale
    )


def local_partner(blocks, stride):
    tok_rows, block_count, width = blocks.shape
    folded = blocks.reshape(tok_rows, block_count // (2 * stride), 2, stride, width)
    return jnp.flip(folded, axis=2).reshape(tok_rows, block_count, width)


def apply_factor(hidden, partner, layer_weights):
    preact = jnp.einsum(
        "tbc,cbd->tbd", hidden, layer_weights[:BLK], preferred_element_type=jnp.float32
    )
    return preact + jnp.einsum(
        "tbc,cbd->tbd", partner, layer_weights[BLK:], preferred_element_type=jnp.float32
    )


def shards(tokens, weights, cotangent):
    tok_rows, local_width = tokens.shape
    blocks_dev = local_width // BLK
    block_bits = (D // BLK).bit_length() - 1
    device_bits = blocks_dev.bit_length() - 1
    data_size = lax.axis_size(("dy", "dz", "dx"))
    grad_scale = 1.0 / math.sqrt(tok_rows * data_size)
    top = FACTORS - 1
    assert block_bits - 1 - device_bits == 1
    cot_blocks = cotangent.reshape(tok_rows, blocks_dev, BLK)
    partner_cot = swapped(cot_blocks, "tensor", 1)
    tokens_f32 = tokens.astype(jnp.float32)
    square_sum = tensor_sum(jnp.sum(tokens_f32 * tokens_f32, axis=1))
    inv_rms = lax.rsqrt(square_sum / D + epsilon)[:, None]
    normed = tokens_f32 * inv_rms
    hidden = normed.astype(jnp.bfloat16).reshape(tok_rows, blocks_dev, BLK)
    stored_inputs = []
    stored_preact = []
    for factor in range(top):
        bit_index = block_bits - FACTORS + factor
        stride = 1 << bit_index
        if stride < blocks_dev:
            partner = local_partner(hidden, stride)
        else:
            partner = swapped(hidden, "tensor", bit_index - device_bits)
        preact = apply_factor(hidden, partner, weights[factor])
        stored_inputs.append((hidden, partner))
        stored_preact.append(preact)
        hidden = gelu_value(preact).astype(jnp.bfloat16)
    hidden, partner_cot = lax.optimization_barrier((hidden, partner_cot))
    partner_top = swapped(hidden, "tensor", 1)
    top_weights = weights[top]
    grad_hidden = jnp.einsum(
        "tbd,cbd->tbc", cot_blocks, top_weights[:BLK], preferred_element_type=jnp.float32
    ) + jnp.einsum(
        "tbd,cbd->tbc",
        partner_cot,
        partner_rows(top_weights[BLK:]),
        preferred_element_type=jnp.float32,
    )
    grad_pre = (grad_hidden * gelu_slope(stored_preact[top - 1])).astype(jnp.bfloat16)
    grad_terms = [None] * FACTORS
    for factor in reversed(range(top)):
        bit_index = block_bits - FACTORS + factor
        stride = 1 << bit_index
        kept_hidden, kept_partner = stored_inputs[factor]
        joined = jnp.concatenate([kept_hidden, kept_partner], axis=2)
        grad_terms[factor] = (exchange_first if factor == 0 else scatter_first)(
            jnp.einsum("tbc,tbd->cbd", joined, grad_pre, preferred_element_type=jnp.float32)
            * grad_scale
        )
        layer_weights = weights[factor]
        near_term = jnp.einsum(
            "tbd,cbd->tbc", grad_pre, layer_weights[:BLK], preferred_element_type=jnp.float32
        )
        far_term = jnp.einsum(
            "tbd,cbd->tbc", grad_pre, layer_weights[BLK:], preferred_element_type=jnp.float32
        )
        if stride < blocks_dev:
            arrived = local_partner(far_term, stride)
        else:
            arrived = swapped(far_term, "tensor", bit_index - device_bits)
        grad_hidden = near_term + arrived
        if factor > 0:
            previous = stored_preact[factor - 1]
            grad_pre = (grad_hidden * gelu_slope(previous)).astype(jnp.bfloat16)
    partner_top, _ = lax.optimization_barrier((partner_top, grad_hidden))
    preact = apply_factor(hidden, partner_top, top_weights)
    mixed = (tokens_f32 + preact.reshape(tok_rows, local_width)).astype(jnp.bfloat16)
    joined = jnp.concatenate([hidden, partner_top], axis=2)
    grad_terms[top] = scatter_first(
        jnp.einsum("tbc,tbd->cbd", joined, cot_blocks, preferred_element_type=jnp.float32)
        * grad_scale
    )
    flat = grad_hidden.reshape(tok_rows, local_width)
    inner_sum = tensor_sum(jnp.sum(flat * normed, axis=1))
    token_grads = (
        cotangent.astype(jnp.float32) + inv_rms * (flat - normed * (inner_sum / D)[:, None])
    ).astype(jnp.bfloat16)
    weight_grads = scatter_rest(grad_terms[1:], grad_terms[0])
    return (mixed, token_grads, weight_grads)


def solution(mesh):
    ny, nz, nx = 4, 4, 4
    fine = Mesh(
        mesh.devices.reshape(ny, nz, nx, mesh.shape["tensor"]), ("dy", "dz", "dx", "tensor")
    )
    dp = ("dy", "dz", "dx")
    return jax.shard_map(
        shards,
        mesh=fine,
        in_specs=(P(dp, "tensor"), P(None, None, "tensor", None), P(dp, "tensor")),
        out_specs=(P(dp, "tensor"), P(dp, "tensor"), P(None, dp, "tensor", None)),
        check_vma=False,
    )
```

```python
import math

import jax
import jax.numpy as jnp
from jax import lax
from jax.sharding import Mesh, PartitionSpec as P

D = 8192
BLK = 256
FACTORS = 3


root_half = 0.7071067811865476
pdf_scale = 0.3989422804014327
epsilon = 1e-06


def swapped(x, axis, stride):
    return lax.ppermute(x, axis, [(i, i ^ 1 << stride) for i in range(lax.axis_size(axis))])


def tensor_sum(x):
    for bit in range(lax.axis_size("tensor").bit_length() - 1):
        x = x + swapped(x, "tensor", bit)
    return x


def scatter_first(grads):
    rows = grads.shape[0]
    ny, nz, nx = (lax.axis_size(a) for a in ("dy", "dz", "dx"))
    rest = grads.shape[1:]
    share = rows // (ny * nz * nx)
    g = lax.psum_scatter(grads.reshape(ny, -1, rest[-1]), "dy", scatter_dimension=0, tiled=True)
    return g.reshape((nz, nx, share) + rest)


def exchange_first(grads):
    rows = grads.shape[0]
    ny, nz, nx = (lax.axis_size(a) for a in ("dy", "dz", "dx"))
    rest = grads.shape[1:]
    g = grads.reshape((ny, nz, nx, rows // (ny * nz * nx)) + rest)
    return jnp.sum(lax.all_to_all(g, "dx", 2, 2), axis=2)


def scatter_rest(on_sc, on_tc):
    nz, nx, share = on_sc[0].shape[:3]
    rest = on_sc[0].shape[3:]
    b = jnp.stack(on_tc, axis=0)
    a, b = lax.optimization_barrier((jnp.stack(on_sc, axis=0), b))
    a = jnp.moveaxis(a, 2, 0)
    a = lax.psum_scatter(a.reshape(nx, -1, rest[-1]), "dx", scatter_dimension=0, tiled=True)
    a = a.reshape((len(on_sc), nz, share) + rest)
    b = jnp.sum(lax.all_to_all(jnp.moveaxis(b, 1, 0), "dy", 0, 0), axis=0)
    g = jnp.moveaxis(jnp.concatenate([b, a], axis=0), 1, 0)
    g = lax.psum_scatter(g.reshape(nz, -1, rest[-1]), "dz", scatter_dimension=0, tiled=True)
    return g.reshape((len(on_tc) + len(on_sc), share) + rest)


def partner_rows(rows):
    pieces = lax.axis_size(("dy", "dx"))
    piece = rows.shape[0] // pieces
    mine = lax.axis_index("dy") * lax.axis_size("dx") + lax.axis_index("dx")
    part = lax.dynamic_slice_in_dim(rows, mine * piece, piece, axis=0)
    part = swapped(part, "tensor", 1)
    return lax.all_gather(part, ("dy", "dx"), axis=0, tiled=True)


def gelu_value(value):
    return value * (0.5 * (1.0 + lax.erf(value * root_half)))


def gelu_slope(value):
    return (
        0.5 * (1.0 + lax.erf(value * root_half)) + value * jnp.exp(-0.5 * value * value) * pdf_scale
    )


def local_partner(blocks, stride):
    tok_rows, block_count, width = blocks.shape
    folded = blocks.reshape(tok_rows, block_count // (2 * stride), 2, stride, width)
    return jnp.flip(folded, axis=2).reshape(tok_rows, block_count, width)


def apply_factor(hidden, partner, layer_weights):
    preact = jnp.einsum(
        "tbc,cbd->tbd", hidden, layer_weights[:BLK], preferred_element_type=jnp.float32
    )
    return preact + jnp.einsum(
        "tbc,cbd->tbd", partner, layer_weights[BLK:], preferred_element_type=jnp.float32
    )


def shards(tokens, weights, cotangent):
    tok_rows, local_width = tokens.shape
    blocks_dev = local_width // BLK
    block_bits = (D // BLK).bit_length() - 1
    device_bits = blocks_dev.bit_length() - 1
    data_size = lax.axis_size(("dy", "dz", "dx"))
    grad_scale = 1.0 / math.sqrt(tok_rows * data_size)
    top = FACTORS - 1
    assert block_bits - 1 - device_bits == 1
    cot_blocks = cotangent.reshape(tok_rows, blocks_dev, BLK)
    partner_cot = swapped(cot_blocks, "tensor", 1)
    tokens_f32 = tokens.astype(jnp.float32)
    square_sum = tensor_sum(jnp.sum(tokens_f32 * tokens_f32, axis=1))
    inv_rms = lax.rsqrt(square_sum / D + epsilon)[:, None]
    normed = tokens_f32 * inv_rms
    hidden = normed.astype(jnp.bfloat16).reshape(tok_rows, blocks_dev, BLK)
    stored_inputs = []
    stored_preact = []
    for factor in range(top):
        bit_index = block_bits - FACTORS + factor
        stride = 1 << bit_index
        if stride < blocks_dev:
            partner = local_partner(hidden, stride)
        else:
            partner = swapped(hidden, "tensor", bit_index - device_bits)
        preact = apply_factor(hidden, partner, weights[factor])
        stored_inputs.append((hidden, partner))
        stored_preact.append(preact)
        hidden = gelu_value(preact).astype(jnp.bfloat16)
    hidden, partner_cot = lax.optimization_barrier((hidden, partner_cot))
    partner_top = swapped(hidden, "tensor", 1)
    top_weights = weights[top]
    grad_hidden = jnp.einsum(
        "tbd,cbd->tbc", cot_blocks, top_weights[:BLK], preferred_element_type=jnp.float32
    ) + jnp.einsum(
        "tbd,cbd->tbc",
        partner_cot,
        partner_rows(top_weights[BLK:]),
        preferred_element_type=jnp.float32,
    )
    grad_pre = (grad_hidden * gelu_slope(stored_preact[top - 1])).astype(jnp.bfloat16)
    grad_terms = [None] * FACTORS
    for factor in reversed(range(top)):
        bit_index = block_bits - FACTORS + factor
        stride = 1 << bit_index
        kept_hidden, kept_partner = stored_inputs[factor]
        joined = jnp.concatenate([kept_hidden, kept_partner], axis=2)
        grad_terms[factor] = exchange_first(
            jnp.einsum("tbc,tbd->cbd", joined, grad_pre, preferred_element_type=jnp.float32)
            * grad_scale
        )
        layer_weights = weights[factor]
        near_term = jnp.einsum(
            "tbd,cbd->tbc", grad_pre, layer_weights[:BLK], preferred_element_type=jnp.float32
        )
        far_term = jnp.einsum(
            "tbd,cbd->tbc", grad_pre, layer_weights[BLK:], preferred_element_type=jnp.float32
        )
        if stride < blocks_dev:
            arrived = local_partner(far_term, stride)
        else:
            arrived = swapped(far_term, "tensor", bit_index - device_bits)
        grad_hidden = near_term + arrived
        if factor > 0:
            previous = stored_preact[factor - 1]
            grad_pre = (grad_hidden * gelu_slope(previous)).astype(jnp.bfloat16)
    partner_top, _, grad_terms[top - 1] = lax.optimization_barrier(
        (partner_top, grad_hidden, grad_terms[top - 1])
    )
    preact = apply_factor(hidden, partner_top, top_weights)
    mixed = (tokens_f32 + preact.reshape(tok_rows, local_width)).astype(jnp.bfloat16)
    joined = jnp.concatenate([hidden, partner_top], axis=2)
    grad_terms[top] = scatter_first(
        jnp.einsum("tbc,tbd->cbd", joined, cot_blocks, preferred_element_type=jnp.float32)
        * grad_scale
    )
    flat = grad_hidden.reshape(tok_rows, local_width)
    inner_sum = tensor_sum(jnp.sum(flat * normed, axis=1))
    token_grads = (
        cotangent.astype(jnp.float32) + inv_rms * (flat - normed * (inner_sum / D)[:, None])
    ).astype(jnp.bfloat16)
    weight_grads = scatter_rest(grad_terms[top:], grad_terms[:top])
    return (mixed, token_grads, weight_grads)


def solution(mesh):
    ny, nz, nx = 4, 4, 4
    fine = Mesh(
        mesh.devices.reshape(ny, nz, nx, mesh.shape["tensor"]), ("dy", "dz", "dx", "tensor")
    )
    dp = ("dy", "dz", "dx")
    return jax.shard_map(
        shards,
        mesh=fine,
        in_specs=(P(dp, "tensor"), P(None, None, "tensor", None), P(dp, "tensor")),
        out_specs=(P(dp, "tensor"), P(dp, "tensor"), P(None, dp, "tensor", None)),
        check_vma=False,
    )
```

```python
import math

import jax
import jax.numpy as jnp
from jax import lax
from jax.sharding import Mesh, PartitionSpec as P

D = 8192
BLK = 256
FACTORS = 3


root_half = 0.7071067811865476
pdf_scale = 0.3989422804014327
epsilon = 1e-06


def swapped(x, axis, stride):
    return lax.ppermute(x, axis, [(i, i ^ 1 << stride) for i in range(lax.axis_size(axis))])


def tensor_sum(x):
    for bit in range(lax.axis_size("tensor").bit_length() - 1):
        x = x + swapped(x, "tensor", bit)
    return x


def scatter_first(grads):
    rows = grads.shape[0]
    ny, nz, nx = (lax.axis_size(a) for a in ("dy", "dz", "dx"))
    rest = grads.shape[1:]
    share = rows // (ny * nz * nx)
    g = lax.psum_scatter(grads.reshape(ny, -1, rest[-1]), "dy", scatter_dimension=0, tiled=True)
    return g.reshape((nz, nx, share) + rest)


def exchange_first(grads):
    rows = grads.shape[0]
    ny, nz, nx = (lax.axis_size(a) for a in ("dy", "dz", "dx"))
    rest = grads.shape[1:]
    g = grads.reshape((ny, nz, nx, rows // (ny * nz * nx)) + rest)
    return jnp.sum(lax.all_to_all(g, "dx", 2, 2), axis=2)


def scatter_rest(on_sc, on_tc, order):
    nz, nx, share = on_sc[0].shape[:3]
    rest = on_sc[0].shape[3:]
    a, b = lax.optimization_barrier((jnp.stack(on_sc, axis=0), jnp.stack(on_tc, axis=0)))
    a = jnp.moveaxis(a, 2, 0)
    a = lax.psum_scatter(a.reshape(nx, -1, rest[-1]), "dx", scatter_dimension=0, tiled=True)
    a = a.reshape((len(on_sc), nz, share) + rest)
    b = jnp.sum(lax.all_to_all(jnp.moveaxis(b, 1, 0), "dy", 0, 0), axis=0)
    g = jnp.concatenate([b, a], axis=0)
    g = jnp.moveaxis(jnp.stack([g[i] for i in order], axis=0), 1, 0)
    g = lax.psum_scatter(g.reshape(nz, -1, rest[-1]), "dz", scatter_dimension=0, tiled=True)
    return g.reshape((len(order), share) + rest)


def partner_rows(rows):
    pieces = lax.axis_size(("dy", "dx"))
    piece = rows.shape[0] // pieces
    mine = lax.axis_index("dy") * lax.axis_size("dx") + lax.axis_index("dx")
    part = lax.dynamic_slice_in_dim(rows, mine * piece, piece, axis=0)
    part = swapped(part, "tensor", 1)
    return lax.all_gather(part, ("dy", "dx"), axis=0, tiled=True)


def gelu_value(value):
    return value * (0.5 * (1.0 + lax.erf(value * root_half)))


def gelu_slope(value):
    return (
        0.5 * (1.0 + lax.erf(value * root_half)) + value * jnp.exp(-0.5 * value * value) * pdf_scale
    )


def local_partner(blocks, stride):
    tok_rows, block_count, width = blocks.shape
    folded = blocks.reshape(tok_rows, block_count // (2 * stride), 2, stride, width)
    return jnp.flip(folded, axis=2).reshape(tok_rows, block_count, width)


def apply_factor(hidden, partner, layer_weights):
    preact = jnp.einsum(
        "tbc,cbd->tbd", hidden, layer_weights[:BLK], preferred_element_type=jnp.float32
    )
    return preact + jnp.einsum(
        "tbc,cbd->tbd", partner, layer_weights[BLK:], preferred_element_type=jnp.float32
    )


def shards(tokens, weights, cotangent):
    tok_rows, local_width = tokens.shape
    blocks_dev = local_width // BLK
    block_bits = (D // BLK).bit_length() - 1
    device_bits = blocks_dev.bit_length() - 1
    data_size = lax.axis_size(("dy", "dz", "dx"))
    grad_scale = 1.0 / math.sqrt(tok_rows * data_size)
    top = FACTORS - 1
    assert block_bits - 1 - device_bits == 1
    cot_blocks = cotangent.reshape(tok_rows, blocks_dev, BLK)
    partner_cot = swapped(cot_blocks, "tensor", 1)
    tokens_f32 = tokens.astype(jnp.float32)
    square_sum = tensor_sum(jnp.sum(tokens_f32 * tokens_f32, axis=1))
    inv_rms = lax.rsqrt(square_sum / D + epsilon)[:, None]
    normed = tokens_f32 * inv_rms
    hidden = normed.astype(jnp.bfloat16).reshape(tok_rows, blocks_dev, BLK)
    stored_inputs = []
    stored_preact = []
    for factor in range(top):
        bit_index = block_bits - FACTORS + factor
        stride = 1 << bit_index
        if stride < blocks_dev:
            partner = local_partner(hidden, stride)
        else:
            partner = swapped(hidden, "tensor", bit_index - device_bits)
        preact = apply_factor(hidden, partner, weights[factor])
        stored_inputs.append((hidden, partner))
        stored_preact.append(preact)
        hidden = gelu_value(preact).astype(jnp.bfloat16)
    hidden, partner_cot = lax.optimization_barrier((hidden, partner_cot))
    partner_top = swapped(hidden, "tensor", 1)
    top_weights = weights[top]
    grad_hidden = jnp.einsum(
        "tbd,cbd->tbc", cot_blocks, top_weights[:BLK], preferred_element_type=jnp.float32
    ) + jnp.einsum(
        "tbd,cbd->tbc",
        partner_cot,
        partner_rows(top_weights[BLK:]),
        preferred_element_type=jnp.float32,
    )
    grad_pre = (grad_hidden * gelu_slope(stored_preact[top - 1])).astype(jnp.bfloat16)
    grad_terms = [None] * FACTORS
    for factor in reversed(range(top)):
        bit_index = block_bits - FACTORS + factor
        stride = 1 << bit_index
        kept_hidden, kept_partner = stored_inputs[factor]
        joined = jnp.concatenate([kept_hidden, kept_partner], axis=2)
        grad_terms[factor] = (exchange_first if factor == 0 else scatter_first)(
            jnp.einsum("tbc,tbd->cbd", joined, grad_pre, preferred_element_type=jnp.float32)
            * grad_scale
        )
        layer_weights = weights[factor]
        near_term = jnp.einsum(
            "tbd,cbd->tbc", grad_pre, layer_weights[:BLK], preferred_element_type=jnp.float32
        )
        far_term = jnp.einsum(
            "tbd,cbd->tbc", grad_pre, layer_weights[BLK:], preferred_element_type=jnp.float32
        )
        if stride < blocks_dev:
            arrived = local_partner(far_term, stride)
        else:
            arrived = swapped(far_term, "tensor", bit_index - device_bits)
        grad_hidden = near_term + arrived
        if factor > 0:
            previous = stored_preact[factor - 1]
            grad_pre = (grad_hidden * gelu_slope(previous)).astype(jnp.bfloat16)
    partner_top, _ = lax.optimization_barrier((partner_top, grad_hidden))
    preact = apply_factor(hidden, partner_top, top_weights)
    mixed = (tokens_f32 + preact.reshape(tok_rows, local_width)).astype(jnp.bfloat16)
    joined = jnp.concatenate([hidden, partner_top], axis=2)
    grad_terms[top] = exchange_first(
        jnp.einsum("tbc,tbd->cbd", joined, cot_blocks, preferred_element_type=jnp.float32)
        * grad_scale
    )
    flat = grad_hidden.reshape(tok_rows, local_width)
    inner_sum = tensor_sum(jnp.sum(flat * normed, axis=1))
    token_grads = (
        cotangent.astype(jnp.float32) + inv_rms * (flat - normed * (inner_sum / D)[:, None])
    ).astype(jnp.bfloat16)
    weight_grads = scatter_rest(
        grad_terms[1:top], [grad_terms[0], grad_terms[top]], [0] + list(range(2, top + 1)) + [1]
    )
    return (mixed, token_grads, weight_grads)


def solution(mesh):
    ny, nz, nx = 4, 4, 4
    fine = Mesh(
        mesh.devices.reshape(ny, nz, nx, mesh.shape["tensor"]), ("dy", "dz", "dx", "tensor")
    )
    dp = ("dy", "dz", "dx")
    return jax.shard_map(
        shards,
        mesh=fine,
        in_specs=(P(dp, "tensor"), P(None, None, "tensor", None), P(dp, "tensor")),
        out_specs=(P(dp, "tensor"), P(dp, "tensor"), P(None, dp, "tensor", None)),
        check_vma=False,
    )
```

```python
import math

import jax
import jax.numpy as jnp
from jax import lax
from jax.sharding import Mesh, PartitionSpec as P

D = 8192
BLK = 256
FACTORS = 3


root_half = 0.7071067811865476
pdf_scale = 0.3989422804014327
epsilon = 1e-06


def swapped(x, axis, stride):
    return lax.ppermute(x, axis, [(i, i ^ 1 << stride) for i in range(lax.axis_size(axis))])


def tensor_sum(x):
    for bit in range(lax.axis_size("tensor").bit_length() - 1):
        x = x + swapped(x, "tensor", bit)
    return x


def scatter_first(grads):
    rows = grads.shape[0]
    ny, nz, nx = (lax.axis_size(a) for a in ("dy", "dz", "dx"))
    rest = grads.shape[1:]
    share = rows // (ny * nz * nx)
    g = lax.psum_scatter(grads.reshape(ny, -1, rest[-1]), "dy", scatter_dimension=0, tiled=True)
    return g.reshape((nz, nx, share) + rest)


def exchange_first(grads):
    rows = grads.shape[0]
    ny, nz, nx = (lax.axis_size(a) for a in ("dy", "dz", "dx"))
    rest = grads.shape[1:]
    g = grads.reshape((ny, nz, nx, rows // (ny * nz * nx)) + rest)
    return jnp.sum(lax.all_to_all(g, "dx", 2, 2), axis=2)


def scatter_rest(on_sc, on_tc):
    nz, nx, share = on_sc[0].shape[:3]
    rest = on_sc[0].shape[3:]
    a, on_tc = lax.optimization_barrier((jnp.stack(on_sc, axis=0), on_tc))
    a = jnp.moveaxis(a, 2, 0)
    a = lax.psum_scatter(a.reshape(nx, -1, rest[-1]), "dx", scatter_dimension=0, tiled=True)
    a = a.reshape((len(on_sc), nz, share) + rest)
    b = jnp.sum(lax.all_to_all(on_tc, "dy", 0, 0), axis=0)
    g = jnp.moveaxis(jnp.concatenate([b[None], a], axis=0), 1, 0)
    return jnp.sum(lax.all_to_all(g, "dz", 0, 0), axis=0)


def partner_rows(rows):
    pieces = lax.axis_size(("dy", "dx"))
    piece = rows.shape[0] // pieces
    mine = lax.axis_index("dy") * lax.axis_size("dx") + lax.axis_index("dx")
    part = lax.dynamic_slice_in_dim(rows, mine * piece, piece, axis=0)
    part = swapped(part, "tensor", 1)
    return lax.all_gather(part, ("dy", "dx"), axis=0, tiled=True)


def gelu_value(value):
    return value * (0.5 * (1.0 + lax.erf(value * root_half)))


def gelu_slope(value):
    return (
        0.5 * (1.0 + lax.erf(value * root_half)) + value * jnp.exp(-0.5 * value * value) * pdf_scale
    )


def local_partner(blocks, stride):
    tok_rows, block_count, width = blocks.shape
    folded = blocks.reshape(tok_rows, block_count // (2 * stride), 2, stride, width)
    return jnp.flip(folded, axis=2).reshape(tok_rows, block_count, width)


def apply_factor(hidden, partner, layer_weights):
    preact = jnp.einsum(
        "tbc,cbd->tbd", hidden, layer_weights[:BLK], preferred_element_type=jnp.float32
    )
    return preact + jnp.einsum(
        "tbc,cbd->tbd", partner, layer_weights[BLK:], preferred_element_type=jnp.float32
    )


def shards(tokens, weights, cotangent):
    tok_rows, local_width = tokens.shape
    blocks_dev = local_width // BLK
    block_bits = (D // BLK).bit_length() - 1
    device_bits = blocks_dev.bit_length() - 1
    data_size = lax.axis_size(("dy", "dz", "dx"))
    grad_scale = 1.0 / math.sqrt(tok_rows * data_size)
    top = FACTORS - 1
    assert block_bits - 1 - device_bits == 1
    cot_blocks = cotangent.reshape(tok_rows, blocks_dev, BLK)
    partner_cot = swapped(cot_blocks, "tensor", 1)
    tokens_f32 = tokens.astype(jnp.float32)
    square_sum = tensor_sum(jnp.sum(tokens_f32 * tokens_f32, axis=1))
    inv_rms = lax.rsqrt(square_sum / D + epsilon)[:, None]
    normed = tokens_f32 * inv_rms
    hidden = normed.astype(jnp.bfloat16).reshape(tok_rows, blocks_dev, BLK)
    stored_inputs = []
    stored_preact = []
    for factor in range(top):
        bit_index = block_bits - FACTORS + factor
        stride = 1 << bit_index
        if stride < blocks_dev:
            partner = local_partner(hidden, stride)
        else:
            partner = swapped(hidden, "tensor", bit_index - device_bits)
        preact = apply_factor(hidden, partner, weights[factor])
        stored_inputs.append((hidden, partner))
        stored_preact.append(preact)
        hidden = gelu_value(preact).astype(jnp.bfloat16)
    hidden, partner_cot = lax.optimization_barrier((hidden, partner_cot))
    partner_top = swapped(hidden, "tensor", 1)
    top_weights = weights[top]
    grad_hidden = jnp.einsum(
        "tbd,cbd->tbc", cot_blocks, top_weights[:BLK], preferred_element_type=jnp.float32
    ) + jnp.einsum(
        "tbd,cbd->tbc",
        partner_cot,
        partner_rows(top_weights[BLK:]),
        preferred_element_type=jnp.float32,
    )
    grad_pre = (grad_hidden * gelu_slope(stored_preact[top - 1])).astype(jnp.bfloat16)
    grad_terms = [None] * FACTORS
    for factor in reversed(range(top)):
        bit_index = block_bits - FACTORS + factor
        stride = 1 << bit_index
        kept_hidden, kept_partner = stored_inputs[factor]
        joined = jnp.concatenate([kept_hidden, kept_partner], axis=2)
        grad_terms[factor] = (exchange_first if factor == 0 else scatter_first)(
            jnp.einsum("tbc,tbd->cbd", joined, grad_pre, preferred_element_type=jnp.float32)
            * grad_scale
        )
        layer_weights = weights[factor]
        near_term = jnp.einsum(
            "tbd,cbd->tbc", grad_pre, layer_weights[:BLK], preferred_element_type=jnp.float32
        )
        far_term = jnp.einsum(
            "tbd,cbd->tbc", grad_pre, layer_weights[BLK:], preferred_element_type=jnp.float32
        )
        if stride < blocks_dev:
            arrived = local_partner(far_term, stride)
        else:
            arrived = swapped(far_term, "tensor", bit_index - device_bits)
        grad_hidden = near_term + arrived
        if factor > 0:
            previous = stored_preact[factor - 1]
            grad_pre = (grad_hidden * gelu_slope(previous)).astype(jnp.bfloat16)
    partner_top, _ = lax.optimization_barrier((partner_top, grad_hidden))
    preact = apply_factor(hidden, partner_top, top_weights)
    mixed = (tokens_f32 + preact.reshape(tok_rows, local_width)).astype(jnp.bfloat16)
    joined = jnp.concatenate([hidden, partner_top], axis=2)
    grad_terms[top] = scatter_first(
        jnp.einsum("tbc,tbd->cbd", joined, cot_blocks, preferred_element_type=jnp.float32)
        * grad_scale
    )
    flat = grad_hidden.reshape(tok_rows, local_width)
    inner_sum = tensor_sum(jnp.sum(flat * normed, axis=1))
    token_grads = (
        cotangent.astype(jnp.float32) + inv_rms * (flat - normed * (inner_sum / D)[:, None])
    ).astype(jnp.bfloat16)
    weight_grads = scatter_rest(grad_terms[1:], grad_terms[0])
    return (mixed, token_grads, weight_grads)


def solution(mesh):
    ny, nz, nx = 4, 4, 4
    fine = Mesh(
        mesh.devices.reshape(ny, nz, nx, mesh.shape["tensor"]), ("dy", "dz", "dx", "tensor")
    )
    dp = ("dy", "dz", "dx")
    return jax.shard_map(
        shards,
        mesh=fine,
        in_specs=(P(dp, "tensor"), P(None, None, "tensor", None), P(dp, "tensor")),
        out_specs=(P(dp, "tensor"), P(dp, "tensor"), P(None, dp, "tensor", None)),
        check_vma=False,
    )
```

```python
import math

import jax
import jax.numpy as jnp
from jax import lax
from jax.sharding import Mesh, PartitionSpec as P

D = 8192
BLK = 256
FACTORS = 3


root_half = 0.7071067811865476
pdf_scale = 0.3989422804014327
epsilon = 1e-06


def swapped(x, axis, stride):
    return lax.ppermute(x, axis, [(i, i ^ 1 << stride) for i in range(lax.axis_size(axis))])


def tensor_sum(x):
    for bit in range(lax.axis_size("tensor").bit_length() - 1):
        x = x + swapped(x, "tensor", bit)
    return x


def scatter_first(grads):
    rows = grads.shape[0]
    ny, nz, nx = (lax.axis_size(a) for a in ("dy", "dz", "dx"))
    rest = grads.shape[1:]
    share = rows // (ny * nz * nx)
    g = lax.psum_scatter(grads.reshape(ny, -1, rest[-1]), "dy", scatter_dimension=0, tiled=True)
    return g.reshape((nz, nx, share) + rest)


def exchange_first(grads):
    rows = grads.shape[0]
    ny, nz, nx = (lax.axis_size(a) for a in ("dy", "dz", "dx"))
    rest = grads.shape[1:]
    g = grads.reshape((ny, nz, nx, rows // (ny * nz * nx)) + rest)
    return jnp.sum(lax.all_to_all(g, "dx", 2, 2), axis=2)


def scatter_rest(on_sc, on_tc):
    nz, nx, share = on_sc[0].shape[:3]
    rest = on_sc[0].shape[3:]
    a, on_tc = lax.optimization_barrier((jnp.stack(on_sc, axis=0), on_tc))
    a = jnp.sum(lax.all_to_all(a, "dx", 2, 2), axis=2)
    b = jnp.sum(lax.all_to_all(on_tc, "dy", 0, 0), axis=0)
    g = jnp.moveaxis(jnp.concatenate([b[None], a], axis=0), 1, 0)
    return jnp.sum(lax.all_to_all(g, "dz", 0, 0), axis=0)


def partner_rows(rows):
    pieces = lax.axis_size(("dy", "dx"))
    piece = rows.shape[0] // pieces
    mine = lax.axis_index("dy") * lax.axis_size("dx") + lax.axis_index("dx")
    part = lax.dynamic_slice_in_dim(rows, mine * piece, piece, axis=0)
    part = swapped(part, "tensor", 1)
    return lax.all_gather(part, ("dy", "dx"), axis=0, tiled=True)


def gelu_value(value):
    return value * (0.5 * (1.0 + lax.erf(value * root_half)))


def gelu_slope(value):
    return (
        0.5 * (1.0 + lax.erf(value * root_half)) + value * jnp.exp(-0.5 * value * value) * pdf_scale
    )


def local_partner(blocks, stride):
    tok_rows, block_count, width = blocks.shape
    folded = blocks.reshape(tok_rows, block_count // (2 * stride), 2, stride, width)
    return jnp.flip(folded, axis=2).reshape(tok_rows, block_count, width)


def apply_factor(hidden, partner, layer_weights):
    preact = jnp.einsum(
        "tbc,cbd->tbd", hidden, layer_weights[:BLK], preferred_element_type=jnp.float32
    )
    return preact + jnp.einsum(
        "tbc,cbd->tbd", partner, layer_weights[BLK:], preferred_element_type=jnp.float32
    )


def shards(tokens, weights, cotangent):
    tok_rows, local_width = tokens.shape
    blocks_dev = local_width // BLK
    block_bits = (D // BLK).bit_length() - 1
    device_bits = blocks_dev.bit_length() - 1
    data_size = lax.axis_size(("dy", "dz", "dx"))
    grad_scale = 1.0 / math.sqrt(tok_rows * data_size)
    top = FACTORS - 1
    assert block_bits - 1 - device_bits == 1
    cot_blocks = cotangent.reshape(tok_rows, blocks_dev, BLK)
    partner_cot = swapped(cot_blocks, "tensor", 1)
    tokens_f32 = tokens.astype(jnp.float32)
    square_sum = tensor_sum(jnp.sum(tokens_f32 * tokens_f32, axis=1))
    inv_rms = lax.rsqrt(square_sum / D + epsilon)[:, None]
    normed = tokens_f32 * inv_rms
    hidden = normed.astype(jnp.bfloat16).reshape(tok_rows, blocks_dev, BLK)
    stored_inputs = []
    stored_preact = []
    for factor in range(top):
        bit_index = block_bits - FACTORS + factor
        stride = 1 << bit_index
        if stride < blocks_dev:
            partner = local_partner(hidden, stride)
        else:
            partner = swapped(hidden, "tensor", bit_index - device_bits)
        preact = apply_factor(hidden, partner, weights[factor])
        stored_inputs.append((hidden, partner))
        stored_preact.append(preact)
        hidden = gelu_value(preact).astype(jnp.bfloat16)
    hidden, partner_cot = lax.optimization_barrier((hidden, partner_cot))
    partner_top = swapped(hidden, "tensor", 1)
    top_weights = weights[top]
    grad_hidden = jnp.einsum(
        "tbd,cbd->tbc", cot_blocks, top_weights[:BLK], preferred_element_type=jnp.float32
    ) + jnp.einsum(
        "tbd,cbd->tbc",
        partner_cot,
        partner_rows(top_weights[BLK:]),
        preferred_element_type=jnp.float32,
    )
    grad_pre = (grad_hidden * gelu_slope(stored_preact[top - 1])).astype(jnp.bfloat16)
    grad_terms = [None] * FACTORS
    for factor in reversed(range(top)):
        bit_index = block_bits - FACTORS + factor
        stride = 1 << bit_index
        kept_hidden, kept_partner = stored_inputs[factor]
        joined = jnp.concatenate([kept_hidden, kept_partner], axis=2)
        grad_terms[factor] = (exchange_first if factor == 0 else scatter_first)(
            jnp.einsum("tbc,tbd->cbd", joined, grad_pre, preferred_element_type=jnp.float32)
            * grad_scale
        )
        layer_weights = weights[factor]
        near_term = jnp.einsum(
            "tbd,cbd->tbc", grad_pre, layer_weights[:BLK], preferred_element_type=jnp.float32
        )
        far_term = jnp.einsum(
            "tbd,cbd->tbc", grad_pre, layer_weights[BLK:], preferred_element_type=jnp.float32
        )
        if stride < blocks_dev:
            arrived = local_partner(far_term, stride)
        else:
            arrived = swapped(far_term, "tensor", bit_index - device_bits)
        grad_hidden = near_term + arrived
        if factor > 0:
            previous = stored_preact[factor - 1]
            grad_pre = (grad_hidden * gelu_slope(previous)).astype(jnp.bfloat16)
    partner_top, _ = lax.optimization_barrier((partner_top, grad_hidden))
    preact = apply_factor(hidden, partner_top, top_weights)
    mixed = (tokens_f32 + preact.reshape(tok_rows, local_width)).astype(jnp.bfloat16)
    joined = jnp.concatenate([hidden, partner_top], axis=2)
    grad_terms[top] = scatter_first(
        jnp.einsum("tbc,tbd->cbd", joined, cot_blocks, preferred_element_type=jnp.float32)
        * grad_scale
    )
    flat = grad_hidden.reshape(tok_rows, local_width)
    inner_sum = tensor_sum(jnp.sum(flat * normed, axis=1))
    token_grads = (
        cotangent.astype(jnp.float32) + inv_rms * (flat - normed * (inner_sum / D)[:, None])
    ).astype(jnp.bfloat16)
    weight_grads = scatter_rest(grad_terms[1:], grad_terms[0])
    return (mixed, token_grads, weight_grads)


def solution(mesh):
    ny, nz, nx = 4, 4, 4
    fine = Mesh(
        mesh.devices.reshape(ny, nz, nx, mesh.shape["tensor"]), ("dy", "dz", "dx", "tensor")
    )
    dp = ("dy", "dz", "dx")
    return jax.shard_map(
        shards,
        mesh=fine,
        in_specs=(P(dp, "tensor"), P(None, None, "tensor", None), P(dp, "tensor")),
        out_specs=(P(dp, "tensor"), P(dp, "tensor"), P(None, dp, "tensor", None)),
        check_vma=False,
    )
```

```python
import math

import jax
import jax.numpy as jnp
from jax import lax
from jax.sharding import Mesh, PartitionSpec as P

D = 8192
BLK = 256
FACTORS = 3


root_half = 0.7071067811865476
pdf_scale = 0.3989422804014327
epsilon = 1e-06


def swapped(x, axis, stride):
    return lax.ppermute(x, axis, [(i, i ^ 1 << stride) for i in range(lax.axis_size(axis))])


def tensor_sum(x):
    for bit in range(lax.axis_size("tensor").bit_length() - 1):
        x = x + swapped(x, "tensor", bit)
    return x


def scatter_first(grads):
    rows = grads.shape[0]
    ny, nz, nx = (lax.axis_size(a) for a in ("dy", "dz", "dx"))
    rest = grads.shape[1:]
    share = rows // (ny * nz * nx)
    g = lax.psum_scatter(grads.reshape(ny, -1, rest[-1]), "dy", scatter_dimension=0, tiled=True)
    return g.reshape((nz, nx, share) + rest)


def exchange_first(grads):
    rows = grads.shape[0]
    ny, nz, nx = (lax.axis_size(a) for a in ("dy", "dz", "dx"))
    rest = grads.shape[1:]
    g = grads.reshape((ny, nz, nx, rows // (ny * nz * nx)) + rest)
    return jnp.sum(lax.all_to_all(g, "dx", 2, 2), axis=2)


def scatter_rest(on_sc, on_tc):
    nz, nx, share = on_sc[0].shape[:3]
    rest = on_sc[0].shape[3:]
    a, on_tc = lax.optimization_barrier((jnp.stack(on_sc, axis=0), on_tc))
    a = jnp.moveaxis(a, 2, 0)
    a = lax.psum_scatter(a.reshape(nx, -1, rest[-1]), "dx", scatter_dimension=0, tiled=True)
    a = a.reshape((len(on_sc), nz, share) + rest)
    b = jnp.sum(lax.all_to_all(on_tc, "dy", 0, 0), axis=0)
    g = jnp.moveaxis(jnp.concatenate([b[None], a], axis=0), 1, 0)
    return jnp.sum(lax.all_to_all(g, "dz", 0, 0), axis=0)


def partner_rows(rows):
    pieces = lax.axis_size(("dy", "dx"))
    piece = rows.shape[0] // pieces
    mine = lax.axis_index("dy") * lax.axis_size("dx") + lax.axis_index("dx")
    part = lax.dynamic_slice_in_dim(rows, mine * piece, piece, axis=0)
    part = swapped(part, "tensor", 1)
    return lax.all_gather(part, ("dy", "dx"), axis=0, tiled=True)


def gelu_value(value):
    return value * (0.5 * (1.0 + lax.erf(value * root_half)))


def gelu_slope(value):
    return (
        0.5 * (1.0 + lax.erf(value * root_half)) + value * jnp.exp(-0.5 * value * value) * pdf_scale
    )


def local_partner(blocks, stride):
    tok_rows, block_count, width = blocks.shape
    folded = blocks.reshape(tok_rows, block_count // (2 * stride), 2, stride, width)
    return jnp.flip(folded, axis=2).reshape(tok_rows, block_count, width)


def apply_factor(hidden, partner, layer_weights):
    preact = jnp.einsum(
        "tbc,cbd->tbd", hidden, layer_weights[:BLK], preferred_element_type=jnp.float32
    )
    return preact + jnp.einsum(
        "tbc,cbd->tbd", partner, layer_weights[BLK:], preferred_element_type=jnp.float32
    )


def shards(tokens, weights, cotangent):
    tok_rows, local_width = tokens.shape
    blocks_dev = local_width // BLK
    block_bits = (D // BLK).bit_length() - 1
    device_bits = blocks_dev.bit_length() - 1
    data_size = lax.axis_size(("dy", "dz", "dx"))
    grad_scale = 1.0 / math.sqrt(tok_rows * data_size)
    top = FACTORS - 1
    assert block_bits - 1 - device_bits == 1
    cot_blocks = cotangent.reshape(tok_rows, blocks_dev, BLK)
    partner_cot = swapped(cot_blocks, "tensor", 1)
    tokens_f32 = tokens.astype(jnp.float32)
    square_sum = tensor_sum(jnp.sum(tokens_f32 * tokens_f32, axis=1))
    inv_rms = lax.rsqrt(square_sum / D + epsilon)[:, None]
    normed = tokens_f32 * inv_rms
    hidden = normed.astype(jnp.bfloat16).reshape(tok_rows, blocks_dev, BLK)
    stored_inputs = []
    stored_preact = []
    for factor in range(top):
        bit_index = block_bits - FACTORS + factor
        stride = 1 << bit_index
        if stride < blocks_dev:
            partner = local_partner(hidden, stride)
        else:
            partner = swapped(hidden, "tensor", bit_index - device_bits)
        preact = apply_factor(hidden, partner, weights[factor])
        stored_inputs.append((hidden, partner))
        stored_preact.append(preact)
        hidden = gelu_value(preact).astype(jnp.bfloat16)
    hidden, partner_cot = lax.optimization_barrier((hidden, partner_cot))
    partner_top = swapped(hidden, "tensor", 1)
    top_weights = weights[top]
    grad_hidden = jnp.einsum(
        "tbd,cbd->tbc", cot_blocks, top_weights[:BLK], preferred_element_type=jnp.float32
    ) + jnp.einsum(
        "tbd,cbd->tbc",
        partner_cot,
        partner_rows(top_weights[BLK:]),
        preferred_element_type=jnp.float32,
    )
    grad_pre = (grad_hidden * gelu_slope(stored_preact[top - 1])).astype(jnp.bfloat16)
    grad_terms = [None] * FACTORS
    for factor in reversed(range(top)):
        bit_index = block_bits - FACTORS + factor
        stride = 1 << bit_index
        kept_hidden, kept_partner = stored_inputs[factor]
        joined = jnp.concatenate([kept_hidden, kept_partner], axis=2)
        grad_terms[factor] = (exchange_first if factor == 0 else scatter_first)(
            jnp.einsum("tbc,tbd->cbd", joined, grad_pre, preferred_element_type=jnp.float32)
            * grad_scale
        )
        layer_weights = weights[factor]
        near_term = jnp.einsum(
            "tbd,cbd->tbc", grad_pre, layer_weights[:BLK], preferred_element_type=jnp.float32
        )
        far_term = jnp.einsum(
            "tbd,cbd->tbc", grad_pre, layer_weights[BLK:], preferred_element_type=jnp.float32
        )
        if stride < blocks_dev:
            arrived = local_partner(far_term, stride)
        else:
            arrived = swapped(far_term, "tensor", bit_index - device_bits)
        grad_hidden = near_term + arrived
        if factor > 0:
            previous = stored_preact[factor - 1]
            grad_pre = (grad_hidden * gelu_slope(previous)).astype(jnp.bfloat16)
    partner_top, _, grad_terms[0] = lax.optimization_barrier(
        (partner_top, grad_hidden, grad_terms[0])
    )
    preact = apply_factor(hidden, partner_top, top_weights)
    mixed = (tokens_f32 + preact.reshape(tok_rows, local_width)).astype(jnp.bfloat16)
    joined = jnp.concatenate([hidden, partner_top], axis=2)
    grad_terms[top] = scatter_first(
        jnp.einsum("tbc,tbd->cbd", joined, cot_blocks, preferred_element_type=jnp.float32)
        * grad_scale
    )
    flat = grad_hidden.reshape(tok_rows, local_width)
    inner_sum = tensor_sum(jnp.sum(flat * normed, axis=1))
    token_grads = (
        cotangent.astype(jnp.float32) + inv_rms * (flat - normed * (inner_sum / D)[:, None])
    ).astype(jnp.bfloat16)
    weight_grads = scatter_rest(grad_terms[1:], grad_terms[0])
    return (mixed, token_grads, weight_grads)


def solution(mesh):
    ny, nz, nx = 4, 4, 4
    fine = Mesh(
        mesh.devices.reshape(ny, nz, nx, mesh.shape["tensor"]), ("dy", "dz", "dx", "tensor")
    )
    dp = ("dy", "dz", "dx")
    return jax.shard_map(
        shards,
        mesh=fine,
        in_specs=(P(dp, "tensor"), P(None, None, "tensor", None), P(dp, "tensor")),
        out_specs=(P(dp, "tensor"), P(dp, "tensor"), P(None, dp, "tensor", None)),
        check_vma=False,
    )
```
